512 devices in a mesh: seq: 64 (over z_hi, y, x), tp: 8 (over z_lo, core).
Axes of the slice: x: 4, y: 8, z: 8 (z_hi: 2, z_lo: 4; z = z_hi * 4 + z_lo), core: 2. Of those that a mesh axis runs over, the one named last changes fastest.
Arguments:
- residual: bfloat16 [16384, 5376], P('seq', 'tp'), may hold values from -10.5 to 10.5
- input_gain: float32 [5376], replicated, may hold values from 0.25 to 1.75
- w_query: bfloat16 [5376, 4096], P('seq', 'tp'), may hold values from -0.078125 to 0.078125
- key_weight: bfloat16 [5376, 2048], P('seq', 'tp'), may hold values from -0.078125 to 0.078125
- value_weight: bfloat16 [5376, 2048], P('seq', 'tp'), may hold values from -0.078125 to 0.078125
- query_gain: float32 [128], replicated, may hold values from 0.25 to 1.75
- key_gain: float32 [128], replicated, may hold values from 0.25 to 1.75
- w_out: bfloat16 [4096, 5376], P('tp', 'seq'), may hold values from -0.1640625 to 0.1640625
- post_gain: float32 [5376], replicated, may hold values from 0.25 to 1.75
- positions: int32 [16384], replicated, may hold values from 0 to 24063, as said below
Outputs:
- mixed: bfloat16 [16384, 5376], P('seq', 'tp')
The draws below stay inside these ranges and needn't reach their ends.
Inputs may be any that keep to these rules, and one draw needn't show every extreme that they name: positions start at 0 and rise by 1 over the first 1024 tokens; after that they rise by 1 or 2 from each token to the next, by 2 at exactly (15360) // 2 tokens.
All inputs are finite; a program needn't handle non-finite values.
Results may differ from the reference program's by a relative error of at most 0.017.
Values may be sent and summed in bfloat16 or wider, within the bound.
No kernel may reach another device: no remote copies, remote signals or barrier semaphores. Data moves between devices by JAX's collectives and lax.ppermute only.
A program may use at most 128 MiB of HBM per device.

```python
import jax
import jax.numpy as jnp
from jax import lax

MODEL_WIDTH = 5376
QUERY_HEADS = 32
KEY_VALUE_HEADS = 16
HEAD_SIZE = 128
LOOKBACK_SPAN = 1024
T_SEQ = 256
DOCUMENT_TOKENS = 16384
N_TP = 8


def column_profile(key, width):
    rise_log = 1.1
    places = jnp.arange(width, dtype=jnp.float32) / width - 0.5
    jitter = jax.random.uniform(key, (width,), jnp.float32, -0.35, 0.35)
    return jnp.exp(rise_log * places + jitter)


def draw_residual(key, part):
    first_key, second_key = jax.random.split(key, 2)
    profile = column_profile(first_key, MODEL_WIDTH)
    value_matrix = jnp.clip(jax.random.normal(second_key, (DOCUMENT_TOKENS, MODEL_WIDTH), jnp.float32), -4.0, 4.0) * profile
    return value_matrix.astype(jnp.bfloat16)


def draw_w_out(key, part):
    first_key, second_key = jax.random.split(key)
    profile = column_profile(first_key, MODEL_WIDTH)
    fan_scale = (QUERY_HEADS * HEAD_SIZE) ** (-0.5)
    base = jnp.clip(jax.random.normal(second_key, (QUERY_HEADS * HEAD_SIZE, MODEL_WIDTH), jnp.float32), -4.0, 4.0)
    return (base * fan_scale * profile).astype(jnp.bfloat16)


def draw_positions(key, part):
    later = DOCUMENT_TOKENS - LOOKBACK_SPAN
    doubled = later // 2
    order = jax.random.permutation(key, later)
    twos = jnp.zeros((later,), jnp.int32).at[order[:doubled]].set(1)
    steps = jnp.concatenate([jnp.zeros((1,), jnp.int32), jnp.ones((LOOKBACK_SPAN - 1,), jnp.int32), 1 + twos])
    return jnp.cumsum(steps).astype(jnp.int32)


def block_scale(stream_key, dims, shards, low, high):
    loudness = 1.0
    for position, parts in shards:
        heights = jax.random.uniform(jax.random.fold_in(jax.random.fold_in(stream_key, 6), position), (parts,), jnp.float32, low / len(shards), high / len(shards))
        loudness = loudness * jnp.repeat(jnp.exp(heights), dims[position] // parts).reshape((-1,) + (1,) * (len(dims) - 1 - position))
    return loudness


def bell_draw(key, dims, scale, reach, cuts=(), kind=jnp.bfloat16):
    level = block_scale(key, dims, cuts, -0.22, 0.18) if cuts else 1.0
    entries = jax.random.normal(key, dims, jnp.float32) * scale * level
    return jnp.minimum(jnp.maximum(entries, -reach), reach).astype(kind)


def setup_inputs(seed: int = 0) -> dict:
    arg_keys = jax.random.split(jax.random.key(seed), 11)
    return {
        "residual": draw_residual(jax.random.fold_in(arg_keys[10], 71), 0),
        "input_gain": jnp.clip(1.0 + 0.15 * jax.random.normal(arg_keys[1], (MODEL_WIDTH,), jnp.float32), 0.25, 1.75),
        "w_query": bell_draw(arg_keys[2], (MODEL_WIDTH, QUERY_HEADS * HEAD_SIZE), MODEL_WIDTH ** -0.5, 0.078125, ((0, 64), (1, 8))),
        "key_weight": bell_draw(arg_keys[3], (MODEL_WIDTH, KEY_VALUE_HEADS * HEAD_SIZE), MODEL_WIDTH ** -0.5, 0.078125, ((0, 64), (1, 8))),
        "value_weight": bell_draw(arg_keys[4], (MODEL_WIDTH, KEY_VALUE_HEADS * HEAD_SIZE), MODEL_WIDTH ** -0.5, 0.078125, ((0, 64), (1, 8))),
        "query_gain": jnp.clip(1.0 + 0.15 * jax.random.normal(arg_keys[5], (HEAD_SIZE,), jnp.float32), 0.25, 1.75),
        "key_gain": jnp.clip(1.0 + 0.15 * jax.random.normal(arg_keys[6], (HEAD_SIZE,), jnp.float32), 0.25, 1.75),
        "w_out": draw_w_out(jax.random.fold_in(arg_keys[10], 71), 0),
        "post_gain": jnp.clip(1.0 + 0.15 * jax.random.normal(arg_keys[8], (MODEL_WIDTH,), jnp.float32), 0.25, 1.75),
        "positions": draw_positions(jax.random.fold_in(arg_keys[10], 71), 0),
    }


epsilon = 1e-06
score_scale = 168.0 ** (-0.5)
rotary_base = 10000.0

def norm_scale(value_matrix, gain):
    mean_square = lax.optimization_barrier(jnp.mean(value_matrix * value_matrix, axis=-1, keepdims=True))
    return value_matrix * lax.rsqrt(mean_square + epsilon) * gain

def rotary(value_matrix, places):
    half_dim = value_matrix.shape[-1] // 2
    inverse = rotary_base ** (-jnp.arange(half_dim, dtype=jnp.float32) / half_dim)
    angles = places.astype(jnp.float32)[:, None] * inverse[None, :]
    cosine = jnp.cos(angles)[:, None, :]
    sine = jnp.sin(angles)[:, None, :]
    first = value_matrix[..., :half_dim]
    second = value_matrix[..., half_dim:]
    return jnp.concatenate([first * cosine - second * sine, second * cosine + first * sine], axis=-1)

def reference(residual, input_gain, w_query, key_weight, value_weight, query_gain, key_gain, w_out, post_gain, positions):
    stream = residual.astype(jnp.float32)
    normalized_input = norm_scale(stream, input_gain).astype(jnp.bfloat16)
    query_group = QUERY_HEADS // KEY_VALUE_HEADS
    queries_raw = jnp.dot(normalized_input, w_query, preferred_element_type=jnp.float32).reshape(DOCUMENT_TOKENS, QUERY_HEADS, HEAD_SIZE)
    unrotated_keys = jnp.dot(normalized_input, key_weight, preferred_element_type=jnp.float32).reshape(DOCUMENT_TOKENS, KEY_VALUE_HEADS, HEAD_SIZE)
    projected_values = jnp.dot(normalized_input, value_weight, preferred_element_type=jnp.float32)
    query_matrix = rotary(norm_scale(queries_raw, query_gain), positions).astype(jnp.bfloat16)
    query_matrix = lax.optimization_barrier(query_matrix).reshape(DOCUMENT_TOKENS, KEY_VALUE_HEADS, query_group, HEAD_SIZE)
    key_matrix = lax.optimization_barrier(rotary(norm_scale(unrotated_keys, key_gain), positions).astype(jnp.bfloat16))
    value_matrix = lax.optimization_barrier(projected_values.astype(jnp.bfloat16)).reshape(DOCUMENT_TOKENS, KEY_VALUE_HEADS, HEAD_SIZE)
    padded_keys = jnp.concatenate([jnp.zeros((LOOKBACK_SPAN, KEY_VALUE_HEADS, HEAD_SIZE), jnp.bfloat16), key_matrix], axis=0)
    padded_values = jnp.concatenate([jnp.zeros((LOOKBACK_SPAN, KEY_VALUE_HEADS, HEAD_SIZE), jnp.bfloat16), value_matrix], axis=0)
    pad_places = jnp.concatenate([jnp.zeros((LOOKBACK_SPAN,), jnp.int32), positions.astype(jnp.int32)])
    pad_index = jnp.arange(DOCUMENT_TOKENS + LOOKBACK_SPAN, dtype=jnp.int32) - LOOKBACK_SPAN
    block_rows = T_SEQ
    span = LOOKBACK_SPAN + block_rows

    def one_block(block_id):
        start = (block_id * block_rows).astype(jnp.int32)
        query_block = lax.dynamic_slice_in_dim(query_matrix, start, block_rows, 0).astype(jnp.float32)
        query_places = lax.dynamic_slice_in_dim(positions.astype(jnp.int32), start, block_rows, 0)
        key_block = lax.dynamic_slice_in_dim(padded_keys, start, span, 0).astype(jnp.float32)
        value_block = lax.dynamic_slice_in_dim(padded_values, start, span, 0).astype(jnp.float32)
        key_places = lax.dynamic_slice_in_dim(pad_places, start, span, 0)
        key_index = lax.dynamic_slice_in_dim(pad_index, start, span, 0)
        distance = query_places[:, None] - key_places[None, :]
        allowed = (key_index[None, :] >= 0) & (distance >= 0) & (distance < LOOKBACK_SPAN)
        scores = jnp.einsum('qkgd,skd->kgqs', query_block, key_block) * score_scale
        weights = jnp.where(allowed[None, None], jnp.exp(scores), jnp.zeros_like(scores))
        total = lax.optimization_barrier(jnp.sum(weights, axis=-1))
        weights_b = lax.optimization_barrier(weights.astype(jnp.bfloat16)).astype(jnp.float32)
        summed = jnp.einsum('kgqs,skd->qkgd', weights_b, value_block)
        attended = summed / jnp.transpose(total, (2, 0, 1))[..., None]
        return attended.astype(jnp.bfloat16).reshape(block_rows, QUERY_HEADS * HEAD_SIZE)
    blocks = lax.map(one_block, jnp.arange(DOCUMENT_TOKENS // block_rows, dtype=jnp.int32))
    attended = blocks.reshape(DOCUMENT_TOKENS, QUERY_HEADS * HEAD_SIZE)
    group_cols = QUERY_HEADS * HEAD_SIZE // N_TP
    split_attended = attended.reshape(DOCUMENT_TOKENS, N_TP, group_cols)
    split_out = w_out.reshape(N_TP, group_cols, MODEL_WIDTH)

    def add_group(carry, index):
        left = lax.dynamic_index_in_dim(split_attended, index, 1, keepdims=False)
        right = lax.dynamic_index_in_dim(split_out, index, 0, keepdims=False)
        part = jnp.dot(left, right, preferred_element_type=jnp.float32).astype(jnp.bfloat16)
        part = lax.optimization_barrier(part)
        return (carry + part.astype(jnp.float32), None)
    attn_sum, _ = lax.scan(add_group, jnp.zeros((DOCUMENT_TOKENS, MODEL_WIDTH), jnp.float32), jnp.arange(N_TP, dtype=jnp.int32))
    return (stream + norm_scale(attn_sum, post_gain)).astype(jnp.bfloat16)
```

```python
import jax
import jax.numpy as jnp
import numpy as np
from jax import lax
from jax.sharding import Mesh
from jax.sharding import PartitionSpec as P

LOOKBACK_SPAN = 1024

SEQ_PARTS = (("zh", 2), ("y", 8), ("x", 4))
TP_PARTS = (("zl", 4), ("c", 2))
SEQ = tuple(name for name, _ in SEQ_PARTS)
TP = tuple(name for name, _ in TP_PARTS)

epsilon = 1e-06
score_scale = 168.0 ** (-0.5)
rotary_base = 10000.0


def from_behind(block, axis, n, distance):
    route = [(i - distance, i) for i in range(n) if i - distance >= 0]
    return lax.ppermute(block, axis, route)


def ring(block, axis, n, split_axis):
    if n == 1:
        return [block]
    fwd = [(i, (i + 1) % n) for i in range(n)]
    bwd = [(i, (i - 1) % n) for i in range(n)]
    if n == 2:
        return [block, lax.ppermute(block, axis, fwd)]
    out = [None] * n
    out[0] = block
    left, right = block, block
    for d in range(1, (n + 1) // 2):
        left = lax.ppermute(left, axis, fwd)
        right = lax.ppermute(right, axis, bwd)
        out[n - d] = left
        out[d] = right
    if n % 2 == 0:
        k = block.shape[split_axis] // 2
        top = lax.ppermute(lax.slice_in_dim(left, 0, k, axis=split_axis), axis, fwd)
        bottom = lax.ppermute(lax.slice_in_dim(right, k, None, axis=split_axis), axis, bwd)
        out[n // 2] = jnp.concatenate([top, bottom], axis=split_axis)
    return out


def gather_axis(block, axis, n, stack_axis, split_axis):
    parts = ring(block, axis, n, split_axis)
    stacked = jnp.stack(parts, axis=stack_axis)
    if n == 1:
        return stacked
    return jnp.roll(stacked, lax.axis_index(axis), axis=stack_axis)


def norm_scale(value_matrix, gain):
    mean_square = jnp.mean(value_matrix * value_matrix, axis=-1, keepdims=True)
    return value_matrix * lax.rsqrt(mean_square + epsilon) * gain


def rotary(value_matrix, places):
    half_dim = value_matrix.shape[-1] // 2
    inverse = rotary_base ** (-jnp.arange(half_dim, dtype=jnp.float32) / half_dim)
    angles = places.astype(jnp.float32)[:, None] * inverse[None, :]
    cosine = jnp.cos(angles)[:, None, :]
    sine = jnp.sin(angles)[:, None, :]
    first = value_matrix[..., :half_dim]
    second = value_matrix[..., half_dim:]
    return jnp.concatenate(
        [first * cosine - second * sine, second * cosine + first * sine], axis=-1
    )


def local(
    residual,
    input_gain,
    w_query,
    key_weight,
    value_weight,
    query_gain,
    key_gain,
    w_out,
    post_gain,
    positions,
):
    sizes = dict(SEQ_PARTS)
    n_seq = int(np.prod([n for _, n in SEQ_PARTS]))
    tok_rows = residual.shape[0]
    seq_at = lax.axis_index(SEQ)
    tp_at = lax.axis_index(TP)
    head_dim = query_gain.shape[0]
    local_kv = key_weight.shape[1] // head_dim
    query_group = w_query.shape[1] // key_weight.shape[1]
    q_cols = w_query.shape[1]
    k_cols = key_weight.shape[1]
    v_cols = value_weight.shape[1]
    shard_rows = w_query.shape[0]

    packed = jnp.concatenate([w_query, key_weight, value_weight, w_out.T], axis=1)
    by_zh = gather_axis(packed, "zh", sizes["zh"], 0, None)
    split = q_cols + k_cols
    half_a = by_zh[:, :, :split]
    half_b = by_zh[:, :, split:]
    a_x = gather_axis(half_a, "x", sizes["x"], 0, 0)
    a_yx = gather_axis(a_x, "y", sizes["y"], 0, 0)
    b_y = gather_axis(half_b, "y", sizes["y"], 0, 0)
    b_yx = gather_axis(b_y, "x", sizes["x"], 1, 0)
    full_rows = n_seq * shard_rows
    a_flat = a_yx.reshape(full_rows, split)
    b_flat = b_yx.reshape(full_rows, half_b.shape[-1])

    gathered = lax.all_gather(residual, TP, axis=1, tiled=True)
    normalized_input = norm_scale(gathered.astype(jnp.float32), input_gain).astype(jnp.bfloat16)
    nz, ny, nx = sizes["zh"], sizes["y"], sizes["x"]
    normed_perm = (
        normalized_input.reshape(tok_rows, nz, ny, nx, shard_rows)
        .transpose(0, 2, 3, 1, 4)
        .reshape(tok_rows, full_rows)
    )
    own_places = lax.dynamic_slice_in_dim(positions, seq_at * tok_rows, tok_rows, 0)
    reach = (LOOKBACK_SPAN - 2) // tok_rows + 1

    def attend(query_matrix, stacked, key_places, valid):
        key_matrix = stacked[0].reshape(-1, local_kv, head_dim)
        value_matrix = stacked[1].reshape(-1, local_kv, head_dim)
        scores = (
            jnp.einsum(
                "qkgd,skd->kgqs", query_matrix, key_matrix, preferred_element_type=jnp.float32
            )
            * score_scale
        )
        distance = own_places[:, None] - key_places[None, :]
        allowed = valid[None, :] & (distance >= 0) & (distance < LOOKBACK_SPAN)
        weights = jnp.where(allowed[None, None], jnp.exp(scores), jnp.zeros_like(scores))
        total = jnp.sum(weights, axis=-1)
        summed = jnp.einsum(
            "kgqs,skd->qkgd",
            weights.astype(jnp.bfloat16),
            value_matrix,
            preferred_element_type=jnp.float32,
        )
        return (total, summed)

    qk = jnp.dot(normed_perm, a_flat, preferred_element_type=jnp.float32)
    queries_raw = qk[:, :q_cols]
    unrotated_keys = qk[:, q_cols:]
    projected_values = jnp.dot(
        normed_perm, b_flat[:, :v_cols], preferred_element_type=jnp.float32
    )
    out_perm = b_flat[:, v_cols:]
    key_matrix = rotary(
        norm_scale(unrotated_keys.reshape(tok_rows, local_kv, head_dim), key_gain), own_places
    )
    stacked = jnp.stack(
        [key_matrix.reshape(tok_rows, local_kv * head_dim), projected_values]
    ).astype(jnp.bfloat16)
    pieces = []
    for distance in range(reach, 0, -1):
        pieces.append(from_behind(stacked, SEQ, n_seq, distance))
    halo = jnp.concatenate(pieces, axis=1)
    query_matrix = rotary(
        norm_scale(queries_raw.reshape(tok_rows, local_kv * query_group, head_dim), query_gain),
        own_places,
    )
    query_matrix = query_matrix.astype(jnp.bfloat16).reshape(
        tok_rows, local_kv, query_group, head_dim
    )
    inner_total, inner_sum = attend(
        query_matrix, stacked, own_places, jnp.ones((tok_rows,), jnp.bool_)
    )
    span = halo.shape[1]
    padded_places = jnp.concatenate([jnp.zeros((span,), jnp.int32), positions])
    halo_places = lax.dynamic_slice_in_dim(padded_places, seq_at * tok_rows, span, 0)
    halo_valid = seq_at * tok_rows - span + jnp.arange(span, dtype=jnp.int32) >= 0
    outer_total, outer_sum = attend(query_matrix, halo, halo_places, halo_valid)
    total = jnp.transpose(inner_total + outer_total, (2, 0, 1))
    merged = (inner_sum + outer_sum) / total[..., None]
    attended = merged.astype(jnp.bfloat16).reshape(tok_rows, local_kv * query_group * head_dim)
    partial_perm = lax.dot_general(
        attended,
        out_perm,
        (((1,), (1,)), ((), ())),
        preferred_element_type=jnp.float32,
    )
    partial_out = (
        partial_perm.reshape(tok_rows, ny, nx, nz, shard_rows)
        .transpose(0, 3, 1, 2, 4)
        .reshape(tok_rows, full_rows)
    )
    summed_cols = lax.psum_scatter(
        partial_out.astype(jnp.bfloat16), TP, scatter_dimension=1, tiled=True
    ).astype(jnp.float32)
    full_width = post_gain.shape[0]
    squares = lax.psum(jnp.sum(summed_cols * summed_cols, axis=1), TP)
    inverse_rms = lax.rsqrt(squares / full_width + epsilon)
    gain_part = lax.dynamic_slice_in_dim(
        post_gain, tp_at * summed_cols.shape[1], summed_cols.shape[1], 0
    )
    return (residual.astype(jnp.float32) + summed_cols * inverse_rms[:, None] * gain_part).astype(
        jnp.bfloat16
    )


def solution(mesh):
    seq_n, tp_n = mesh.devices.shape
    shape = tuple(n for _, n in SEQ_PARTS) + tuple(n for _, n in TP_PARTS)
    assert int(np.prod(shape[:3])) == seq_n and int(np.prod(shape[3:])) == tp_n
    fine = Mesh(mesh.devices.reshape(shape), SEQ + TP)
    blocked = P(SEQ, TP)
    in_specs = (
        blocked,
        P(),
        blocked,
        blocked,
        blocked,
        P(),
        P(),
        P(TP, SEQ),
        P(),
        P(),
    )
    return jax.shard_map(local, mesh=fine, in_specs=in_specs, out_specs=blocked, check_vma=False)
```

```python
import jax
import jax.numpy as jnp
import numpy as np
from jax import lax
from jax.sharding import Mesh
from jax.sharding import PartitionSpec as P

LOOKBACK_SPAN = 1024

SEQ_PARTS = (("zh", 2), ("y", 8), ("x", 4))
TP_PARTS = (("zl", 4), ("c", 2))
SEQ = tuple(name for name, _ in SEQ_PARTS)
TP = tuple(name for name, _ in TP_PARTS)

epsilon = 1e-06
score_scale = 168.0 ** (-0.5)
rotary_base = 10000.0


def from_behind(block, axis, n, distance):
    route = [(i - distance, i) for i in range(n) if i - distance >= 0]
    return lax.ppermute(block, axis, route)


def ring(block, axis, n, split_axis):
    if n == 1:
        return [block]
    fwd = [(i, (i + 1) % n) for i in range(n)]
    bwd = [(i, (i - 1) % n) for i in range(n)]
    if n == 2:
        return [block, lax.ppermute(block, axis, fwd)]
    out = [None] * n
    out[0] = block
    left, right = block, block
    for d in range(1, (n + 1) // 2):
        left = lax.ppermute(left, axis, fwd)
        right = lax.ppermute(right, axis, bwd)
        out[n - d] = left
        out[d] = right
    if n % 2 == 0:
        k = block.shape[split_axis] // 2
        top = lax.ppermute(lax.slice_in_dim(left, 0, k, axis=split_axis), axis, fwd)
        bottom = lax.ppermute(lax.slice_in_dim(right, k, None, axis=split_axis), axis, bwd)
        out[n // 2] = (top, bottom)
    return out


def stacked_ring(block, axis, n, split_axis):
    parts = ring(block, axis, n, split_axis)
    whole = [jnp.concatenate(p, axis=split_axis) if isinstance(p, tuple) else p for p in parts]
    return jnp.stack(whole, axis=0)


def ring_pieces(block, axis, n, split_axis):
    parts = ring(block, axis, n, split_axis)
    full = block.shape[split_axis]
    pieces = []
    for d, p in enumerate(parts):
        if isinstance(p, tuple):
            k = p[0].shape[split_axis]
            pieces.append((d, 0, k, p[0]))
            pieces.append((d, k, full, p[1]))
        else:
            pieces.append((d, 0, full, p))
    return pieces


def norm_scale(value_matrix, gain):
    mean_square = jnp.mean(value_matrix * value_matrix, axis=-1, keepdims=True)
    return value_matrix * lax.rsqrt(mean_square + epsilon) * gain


def rotary(value_matrix, places):
    half_dim = value_matrix.shape[-1] // 2
    inverse = rotary_base ** (-jnp.arange(half_dim, dtype=jnp.float32) / half_dim)
    angles = places.astype(jnp.float32)[:, None] * inverse[None, :]
    cosine = jnp.cos(angles)[:, None, :]
    sine = jnp.sin(angles)[:, None, :]
    first = value_matrix[..., :half_dim]
    second = value_matrix[..., half_dim:]
    return jnp.concatenate(
        [first * cosine - second * sine, second * cosine + first * sine], axis=-1
    )


def local(
    residual,
    input_gain,
    w_query,
    key_weight,
    value_weight,
    query_gain,
    key_gain,
    w_out,
    post_gain,
    positions,
):
    sizes = dict(SEQ_PARTS)
    n_seq = int(np.prod([n for _, n in SEQ_PARTS]))
    tok_rows = residual.shape[0]
    seq_at = lax.axis_index(SEQ)
    tp_at = lax.axis_index(TP)
    head_dim = query_gain.shape[0]
    local_kv = key_weight.shape[1] // head_dim
    query_group = w_query.shape[1] // key_weight.shape[1]
    q_cols = w_query.shape[1]
    k_cols = key_weight.shape[1]
    v_cols = value_weight.shape[1]
    shard_rows = w_query.shape[0]

    nz, ny, nx = sizes["zh"], sizes["y"], sizes["x"]
    packed = jnp.concatenate([w_query, key_weight, value_weight, w_out.T], axis=1)
    by_zh = stacked_ring(packed, "zh", nz, 0)
    split = q_cols + k_cols
    half_a = by_zh[:, :, :split]
    half_b = by_zh[:, :, split:]
    a_x = stacked_ring(half_a, "x", nx, 0)
    a_pieces = ring_pieces(a_x, "y", ny, 0)
    b_y = stacked_ring(half_b, "y", ny, 0)
    b_pieces = ring_pieces(b_y, "x", nx, 0)

    gathered = lax.all_gather(residual, TP, axis=1, tiled=True)
    normalized_input = norm_scale(gathered.astype(jnp.float32), input_gain).astype(jnp.bfloat16)
    at_zh, at_y, at_x = (lax.axis_index(name) for name in SEQ)
    normed_rel = normalized_input.reshape(tok_rows, nz, ny, nx, shard_rows).transpose(0, 2, 3, 1, 4)
    normed_rel = jnp.roll(normed_rel, -at_y, axis=1)
    normed_rel = jnp.roll(normed_rel, -at_x, axis=2)
    normed_rel = jnp.roll(normed_rel, -at_zh, axis=3)

    def contract(lhs, piece):
        return lax.dot_general(
            lhs, piece, (((1, 2, 3), (0, 1, 2)), ((), ())), preferred_element_type=jnp.float32
        )

    qk = None
    for dy, lo, hi, piece in a_pieces:
        term = contract(normed_rel[:, dy, lo:hi], piece)
        qk = term if qk is None else qk + term
    projected_values = None
    for dx, lo, hi, piece in b_pieces:
        term = contract(normed_rel[:, lo:hi, dx], piece[..., :v_cols])
        projected_values = term if projected_values is None else projected_values + term
    queries_raw = qk[:, :q_cols]
    unrotated_keys = qk[:, q_cols:]
    own_places = lax.dynamic_slice_in_dim(positions, seq_at * tok_rows, tok_rows, 0)
    reach = (LOOKBACK_SPAN - 2) // tok_rows + 1

    def attend(query_matrix, stacked, key_places, valid):
        key_matrix = stacked[0].reshape(-1, local_kv, head_dim)
        value_matrix = stacked[1].reshape(-1, local_kv, head_dim)
        scores = (
            jnp.einsum(
                "qkgd,skd->kgqs", query_matrix, key_matrix, preferred_element_type=jnp.float32
            )
            * score_scale
        )
        distance = own_places[:, None] - key_places[None, :]
        allowed = valid[None, :] & (distance >= 0) & (distance < LOOKBACK_SPAN)
        weights = jnp.where(allowed[None, None], jnp.exp(scores), jnp.zeros_like(scores))
        total = jnp.sum(weights, axis=-1)
        summed = jnp.einsum(
            "kgqs,skd->qkgd",
            weights.astype(jnp.bfloat16),
            value_matrix,
            preferred_element_type=jnp.float32,
        )
        return (total, summed)

    key_matrix = rotary(
        norm_scale(unrotated_keys.reshape(tok_rows, local_kv, head_dim), key_gain), own_places
    )
    stacked = jnp.stack(
        [key_matrix.reshape(tok_rows, local_kv * head_dim), projected_values]
    ).astype(jnp.bfloat16)
    pieces = []
    for distance in range(reach, 0, -1):
        pieces.append(from_behind(stacked, SEQ, n_seq, distance))
    halo = jnp.concatenate(pieces, axis=1)
    query_matrix = rotary(
        norm_scale(queries_raw.reshape(tok_rows, local_kv * query_group, head_dim), query_gain),
        own_places,
    )
    query_matrix = query_matrix.astype(jnp.bfloat16).reshape(
        tok_rows, local_kv, query_group, head_dim
    )
    inner_total, inner_sum = attend(
        query_matrix, stacked, own_places, jnp.ones((tok_rows,), jnp.bool_)
    )
    span = halo.shape[1]
    padded_places = jnp.concatenate([jnp.zeros((span,), jnp.int32), positions])
    halo_places = lax.dynamic_slice_in_dim(padded_places, seq_at * tok_rows, span, 0)
    halo_valid = seq_at * tok_rows - span + jnp.arange(span, dtype=jnp.int32) >= 0
    outer_total, outer_sum = attend(query_matrix, halo, halo_places, halo_valid)
    total = jnp.transpose(inner_total + outer_total, (2, 0, 1))
    merged = (inner_sum + outer_sum) / total[..., None]
    attended = merged.astype(jnp.bfloat16).reshape(tok_rows, local_kv * query_group * head_dim)
    out_rel = jnp.zeros((tok_rows, ny, nx, nz, shard_rows), jnp.bfloat16)
    for dx, lo, hi, piece in b_pieces:
        cols = lax.dot_general(
            attended,
            piece[..., v_cols:],
            (((1,), (3,)), ((), ())),
            preferred_element_type=jnp.float32,
        )
        out_rel = out_rel.at[:, lo:hi, dx].set(cols.astype(jnp.bfloat16))
    out_abs = jnp.roll(out_rel, at_y, axis=1)
    out_abs = jnp.roll(out_abs, at_x, axis=2)
    out_abs = jnp.roll(out_abs, at_zh, axis=3)
    partial_out = out_abs.transpose(0, 3, 1, 2, 4).reshape(tok_rows, n_seq * shard_rows)
    summed_cols = lax.psum_scatter(
        partial_out, TP, scatter_dimension=1, tiled=True
    ).astype(jnp.float32)
    full_width = post_gain.shape[0]
    squares = lax.psum(jnp.sum(summed_cols * summed_cols, axis=1), TP)
    inverse_rms = lax.rsqrt(squares / full_width + epsilon)
    gain_part = lax.dynamic_slice_in_dim(
        post_gain, tp_at * summed_cols.shape[1], summed_cols.shape[1], 0
    )
    return (residual.astype(jnp.float32) + summed_cols * inverse_rms[:, None] * gain_part).astype(
        jnp.bfloat16
    )


def solution(mesh):
    seq_n, tp_n = mesh.devices.shape
    shape = tuple(n for _, n in SEQ_PARTS) + tuple(n for _, n in TP_PARTS)
    assert int(np.prod(shape[:3])) == seq_n and int(np.prod(shape[3:])) == tp_n
    fine = Mesh(mesh.devices.reshape(shape), SEQ + TP)
    blocked = P(SEQ, TP)
    in_specs = (
        blocked,
        P(),
        blocked,
        blocked,
        blocked,
        P(),
        P(),
        P(TP, SEQ),
        P(),
        P(),
    )
    return jax.shard_map(local, mesh=fine, in_specs=in_specs, out_specs=blocked, check_vma=False)
```

```python
import jax
import jax.numpy as jnp
import numpy as np
from jax import lax
from jax.sharding import Mesh
from jax.sharding import PartitionSpec as P

LOOKBACK_SPAN = 1024

SEQ_PARTS = (("zh", 2), ("y", 8), ("x", 4))
TP_PARTS = (("zl", 4), ("c", 2))
SEQ = tuple(name for name, _ in SEQ_PARTS)
TP = tuple(name for name, _ in TP_PARTS)

epsilon = 1e-06
score_scale = 168.0 ** (-0.5)
rotary_base = 10000.0


def from_behind(block, axis, n, distance):
    route = [(i - distance, i) for i in range(n) if i - distance >= 0]
    return lax.ppermute(block, axis, route)


def ring(block, axis, n, split_axis):
    if n == 1:
        return [block]
    fwd = [(i, (i + 1) % n) for i in range(n)]
    bwd = [(i, (i - 1) % n) for i in range(n)]
    if n == 2:
        return [block, lax.ppermute(block, axis, fwd)]
    out = [None] * n
    out[0] = block
    left, right = block, block
    for d in range(1, (n + 1) // 2):
        left = lax.ppermute(left, axis, fwd)
        right = lax.ppermute(right, axis, bwd)
        out[n - d] = left
        out[d] = right
    if n % 2 == 0:
        k = block.shape[split_axis] // 2
        top = lax.ppermute(lax.slice_in_dim(left, 0, k, axis=split_axis), axis, fwd)
        bottom = lax.ppermute(lax.slice_in_dim(right, k, None, axis=split_axis), axis, bwd)
        out[n // 2] = (top, bottom)
    return out


def stacked_ring(block, axis, n, split_axis):
    parts = ring(block, axis, n, split_axis)
    whole = [jnp.concatenate(p, axis=split_axis) if isinstance(p, tuple) else p for p in parts]
    return jnp.stack(whole, axis=0)


def ring_pieces(block, axis, n, split_axis):
    parts = ring(block, axis, n, split_axis)
    full = block.shape[split_axis]
    pieces = []
    for d, p in enumerate(parts):
        if isinstance(p, tuple):
            k = p[0].shape[split_axis]
            pieces.append((d, 0, k, p[0]))
            pieces.append((d, k, full, p[1]))
        else:
            pieces.append((d, 0, full, p))
    return pieces


def reduce_scatter_tp(partial, n_chip):
    rows = partial.shape[0]
    block_cols = partial.shape[1] // (2 * n_chip)
    at_c = lax.axis_index("c")
    at_z = lax.axis_index("zl")
    blocks = partial.reshape(rows, n_chip, 2, block_cols)
    keep = lax.dynamic_index_in_dim(blocks, at_c, axis=2, keepdims=False)
    give = lax.dynamic_index_in_dim(blocks, 1 - at_c, axis=2, keepdims=False)
    got = lax.ppermute(give, "c", [(0, 1), (1, 0)])
    chip_sum = keep.astype(jnp.float32) + got.astype(jnp.float32)
    rightward = [(i, i + 1) for i in range(n_chip - 1)]
    leftward = [(i + 1, i) for i in range(n_chip - 1)]
    from_left = jnp.zeros((rows, block_cols), jnp.float32)
    from_right = jnp.zeros((rows, block_cols), jnp.float32)
    for step in range(1, n_chip):
        to_right = jnp.minimum(at_z + n_chip - step, n_chip - 1)
        to_left = jnp.maximum(at_z - n_chip + step, 0)
        send_r = lax.dynamic_index_in_dim(chip_sum, to_right, axis=1, keepdims=False) + from_left
        send_l = lax.dynamic_index_in_dim(chip_sum, to_left, axis=1, keepdims=False) + from_right
        from_left = lax.ppermute(send_r.astype(jnp.bfloat16), "zl", rightward).astype(jnp.float32)
        from_right = lax.ppermute(send_l.astype(jnp.bfloat16), "zl", leftward).astype(jnp.float32)
    own = lax.dynamic_index_in_dim(chip_sum, at_z, axis=1, keepdims=False)
    return own + from_left + from_right


def norm_scale(value_matrix, gain):
    mean_square = jnp.mean(value_matrix * value_matrix, axis=-1, keepdims=True)
    return value_matrix * lax.rsqrt(mean_square + epsilon) * gain


def rotary(value_matrix, places):
    half_dim = value_matrix.shape[-1] // 2
    inverse = rotary_base ** (-jnp.arange(half_dim, dtype=jnp.float32) / half_dim)
    angles = places.astype(jnp.float32)[:, None] * inverse[None, :]
    cosine = jnp.cos(angles)[:, None, :]
    sine = jnp.sin(angles)[:, None, :]
    first = value_matrix[..., :half_dim]
    second = value_matrix[..., half_dim:]
    return jnp.concatenate(
        [first * cosine - second * sine, second * cosine + first * sine], axis=-1
    )


def local(
    residual,
    input_gain,
    w_query,
    key_weight,
    value_weight,
    query_gain,
    key_gain,
    w_out,
    post_gain,
    positions,
):
    sizes = dict(SEQ_PARTS)
    n_seq = int(np.prod([n for _, n in SEQ_PARTS]))
    tok_rows = residual.shape[0]
    seq_at = lax.axis_index(SEQ)
    tp_at = lax.axis_index(TP)
    head_dim = query_gain.shape[0]
    local_kv = key_weight.shape[1] // head_dim
    query_group = w_query.shape[1] // key_weight.shape[1]
    q_cols = w_query.shape[1]
    k_cols = key_weight.shape[1]
    v_cols = value_weight.shape[1]
    shard_rows = w_query.shape[0]

    nz, ny, nx = sizes["zh"], sizes["y"], sizes["x"]
    packed = jnp.concatenate([w_query, key_weight, value_weight, w_out.T], axis=1)
    by_zh = stacked_ring(packed, "zh", nz, 0)
    split = q_cols + k_cols
    half_a = by_zh[:, :, :split]
    half_b = by_zh[:, :, split:]
    a_x = stacked_ring(half_a, "x", nx, 0)
    a_pieces = ring_pieces(a_x, "y", ny, 0)
    b_y = stacked_ring(half_b, "y", ny, 0)
    b_pieces = ring_pieces(b_y, "x", nx, 0)

    gathered = lax.all_gather(residual, TP, axis=1, tiled=True)
    normalized_input = norm_scale(gathered.astype(jnp.float32), input_gain).astype(jnp.bfloat16)
    at_zh, at_y, at_x = (lax.axis_index(name) for name in SEQ)
    normed_rel = normalized_input.reshape(tok_rows, nz, ny, nx, shard_rows).transpose(0, 2, 3, 1, 4)
    normed_rel = jnp.roll(normed_rel, -at_y, axis=1)
    normed_rel = jnp.roll(normed_rel, -at_x, axis=2)
    normed_rel = jnp.roll(normed_rel, -at_zh, axis=3)

    def contract(lhs, piece):
        return lax.dot_general(
            lhs, piece, (((1, 2, 3), (0, 1, 2)), ((), ())), preferred_element_type=jnp.float32
        )

    qk = None
    for dy, lo, hi, piece in a_pieces:
        term = contract(normed_rel[:, dy, lo:hi], piece)
        qk = term if qk is None else qk + term
    projected_values = None
    for dx, lo, hi, piece in b_pieces:
        term = contract(normed_rel[:, lo:hi, dx], piece[..., :v_cols])
        projected_values = term if projected_values is None else projected_values + term
    queries_raw = qk[:, :q_cols]
    unrotated_keys = qk[:, q_cols:]
    own_places = lax.dynamic_slice_in_dim(positions, seq_at * tok_rows, tok_rows, 0)
    reach = (LOOKBACK_SPAN - 2) // tok_rows + 1

    def attend(query_matrix, stacked, key_places, valid):
        key_matrix = stacked[0].reshape(-1, local_kv, head_dim)
        value_matrix = stacked[1].reshape(-1, local_kv, head_dim)
        scores = (
            jnp.einsum(
                "qkgd,skd->kgqs", query_matrix, key_matrix, preferred_element_type=jnp.float32
            )
            * score_scale
        )
        distance = own_places[:, None] - key_places[None, :]
        allowed = valid[None, :] & (distance >= 0) & (distance < LOOKBACK_SPAN)
        weights = jnp.where(allowed[None, None], jnp.exp(scores), jnp.zeros_like(scores))
        total = jnp.sum(weights, axis=-1)
        summed = jnp.einsum(
            "kgqs,skd->qkgd",
            weights.astype(jnp.bfloat16),
            value_matrix,
            preferred_element_type=jnp.float32,
        )
        return (total, summed)

    key_matrix = rotary(
        norm_scale(unrotated_keys.reshape(tok_rows, local_kv, head_dim), key_gain), own_places
    )
    stacked = jnp.stack(
        [key_matrix.reshape(tok_rows, local_kv * head_dim), projected_values]
    ).astype(jnp.bfloat16)
    pieces = []
    for distance in range(reach, 0, -1):
        pieces.append(from_behind(stacked, SEQ, n_seq, distance))
    halo = jnp.concatenate(pieces, axis=1)
    query_matrix = rotary(
        norm_scale(queries_raw.reshape(tok_rows, local_kv * query_group, head_dim), query_gain),
        own_places,
    )
    query_matrix = query_matrix.astype(jnp.bfloat16).reshape(
        tok_rows, local_kv, query_group, head_dim
    )
    inner_total, inner_sum = attend(
        query_matrix, stacked, own_places, jnp.ones((tok_rows,), jnp.bool_)
    )
    span = halo.shape[1]
    padded_places = jnp.concatenate([jnp.zeros((span,), jnp.int32), positions])
    halo_places = lax.dynamic_slice_in_dim(padded_places, seq_at * tok_rows, span, 0)
    halo_valid = seq_at * tok_rows - span + jnp.arange(span, dtype=jnp.int32) >= 0
    outer_total, outer_sum = attend(query_matrix, halo, halo_places, halo_valid)
    total = jnp.transpose(inner_total + outer_total, (2, 0, 1))
    merged = (inner_sum + outer_sum) / total[..., None]
    attended = merged.astype(jnp.bfloat16).reshape(tok_rows, local_kv * query_group * head_dim)
    out_rel = jnp.zeros((tok_rows, ny, nx, nz, shard_rows), jnp.bfloat16)
    for dx, lo, hi, piece in b_pieces:
        cols = lax.dot_general(
            attended,
            piece[..., v_cols:],
            (((1,), (3,)), ((), ())),
            preferred_element_type=jnp.float32,
        )
        out_rel = out_rel.at[:, lo:hi, dx].set(cols.astype(jnp.bfloat16))
    out_abs = jnp.roll(out_rel, at_y, axis=1)
    out_abs = jnp.roll(out_abs, at_x, axis=2)
    out_abs = jnp.roll(out_abs, at_zh, axis=3)
    partial_out = out_abs.transpose(0, 3, 1, 2, 4).reshape(tok_rows, n_seq * shard_rows)
    summed_cols = reduce_scatter_tp(partial_out, dict(TP_PARTS)["zl"])
    full_width = post_gain.shape[0]
    squares = lax.psum(jnp.sum(summed_cols * summed_cols, axis=1), TP)
    inverse_rms = lax.rsqrt(squares / full_width + epsilon)
    gain_part = lax.dynamic_slice_in_dim(
        post_gain, tp_at * summed_cols.shape[1], summed_cols.shape[1], 0
    )
    return (residual.astype(jnp.float32) + summed_cols * inverse_rms[:, None] * gain_part).astype(
        jnp.bfloat16
    )


def solution(mesh):
    seq_n, tp_n = mesh.devices.shape
    shape = tuple(n for _, n in SEQ_PARTS) + tuple(n for _, n in TP_PARTS)
    assert int(np.prod(shape[:3])) == seq_n and int(np.prod(shape[3:])) == tp_n
    fine = Mesh(mesh.devices.reshape(shape), SEQ + TP)
    blocked = P(SEQ, TP)
    in_specs = (
        blocked,
        P(),
        blocked,
        blocked,
        blocked,
        P(),
        P(),
        P(TP, SEQ),
        P(),
        P(),
    )
    return jax.shard_map(local, mesh=fine, in_specs=in_specs, out_specs=blocked, check_vma=False)
```

```python
import jax
import jax.numpy as jnp
import numpy as np
from jax import lax
from jax.sharding import Mesh
from jax.sharding import PartitionSpec as P

LOOKBACK_SPAN = 1024

SEQ_PARTS = (("zh", 2), ("y", 8), ("x", 4))
TP_PARTS = (("zl", 4), ("c", 2))
SEQ = tuple(name for name, _ in SEQ_PARTS)
TP = tuple(name for name, _ in TP_PARTS)

epsilon = 1e-06
score_scale = 168.0 ** (-0.5)
rotary_base = 10000.0


def from_behind(block, axis, n, distance):
    route = [(i - distance, i) for i in range(n) if i - distance >= 0]
    return lax.ppermute(block, axis, route)


def ring(block, axis, n, split_axis):
    if n == 1:
        return [block]
    fwd = [(i, (i + 1) % n) for i in range(n)]
    bwd = [(i, (i - 1) % n) for i in range(n)]
    if n == 2:
        return [block, lax.ppermute(block, axis, fwd)]
    out = [None] * n
    out[0] = block
    left, right = block, block
    for d in range(1, (n + 1) // 2):
        left = lax.ppermute(left, axis, fwd)
        right = lax.ppermute(right, axis, bwd)
        out[n - d] = left
        out[d] = right
    if n % 2 == 0:
        k = block.shape[split_axis] // 2
        top = lax.ppermute(lax.slice_in_dim(left, 0, k, axis=split_axis), axis, fwd)
        bottom = lax.ppermute(lax.slice_in_dim(right, k, None, axis=split_axis), axis, bwd)
        out[n // 2] = (top, bottom)
    return out


def stacked_ring(block, axis, n, split_axis):
    parts = ring(block, axis, n, split_axis)
    whole = [jnp.concatenate(p, axis=split_axis) if isinstance(p, tuple) else p for p in parts]
    return jnp.stack(whole, axis=0)


def ring_pieces(block, axis, n, split_axis, fold=None, acc=None):
    fwd = [(i, (i + 1) % n) for i in range(n)]
    bwd = [(i, (i - 1) % n) for i in range(n)]
    full = block.shape[split_axis]
    pieces = []

    def take(new):
        nonlocal acc
        pieces.extend(new)
        if fold is not None:
            acc = fold(acc, new)

    take([(0, 0, full, block)])
    left, right = block, block
    for d in range(1, (n + 1) // 2):
        if d > 1 and fold is not None:
            left, right, acc = lax.optimization_barrier((left, right, acc))
        left = lax.ppermute(left, axis, fwd)
        right = lax.ppermute(right, axis, bwd)
        take([(n - d, 0, full, left), (d, 0, full, right)])
    if n % 2 == 0:
        if fold is not None:
            left, right, acc = lax.optimization_barrier((left, right, acc))
        k = full // 2
        top = lax.ppermute(lax.slice_in_dim(left, 0, k, axis=split_axis), axis, fwd)
        bottom = lax.ppermute(lax.slice_in_dim(right, k, None, axis=split_axis), axis, bwd)
        take([(n // 2, 0, k, top), (n // 2, k, full, bottom)])
    return pieces, acc


def norm_scale(value_matrix, gain):
    mean_square = jnp.mean(value_matrix * value_matrix, axis=-1, keepdims=True)
    return value_matrix * lax.rsqrt(mean_square + epsilon) * gain


def rotary(value_matrix, places):
    half_dim = value_matrix.shape[-1] // 2
    inverse = rotary_base ** (-jnp.arange(half_dim, dtype=jnp.float32) / half_dim)
    angles = places.astype(jnp.float32)[:, None] * inverse[None, :]
    cosine = jnp.cos(angles)[:, None, :]
    sine = jnp.sin(angles)[:, None, :]
    first = value_matrix[..., :half_dim]
    second = value_matrix[..., half_dim:]
    return jnp.concatenate(
        [first * cosine - second * sine, second * cosine + first * sine], axis=-1
    )


def local(
    residual,
    input_gain,
    w_query,
    key_weight,
    value_weight,
    query_gain,
    key_gain,
    w_out,
    post_gain,
    positions,
):
    sizes = dict(SEQ_PARTS)
    n_seq = int(np.prod([n for _, n in SEQ_PARTS]))
    tok_rows = residual.shape[0]
    seq_at = lax.axis_index(SEQ)
    tp_at = lax.axis_index(TP)
    head_dim = query_gain.shape[0]
    local_kv = key_weight.shape[1] // head_dim
    query_group = w_query.shape[1] // key_weight.shape[1]
    q_cols = w_query.shape[1]
    k_cols = key_weight.shape[1]
    v_cols = value_weight.shape[1]
    shard_rows = w_query.shape[0]

    nz, ny, nx = sizes["zh"], sizes["y"], sizes["x"]
    gathered = lax.all_gather(residual, TP, axis=1, tiled=True)
    normalized_input = norm_scale(gathered.astype(jnp.float32), input_gain).astype(jnp.bfloat16)
    at_zh, at_y, at_x = (lax.axis_index(name) for name in SEQ)
    normed_rel = normalized_input.reshape(tok_rows, nz, ny, nx, shard_rows).transpose(0, 2, 3, 1, 4)
    normed_rel = jnp.roll(normed_rel, -at_y, axis=1)
    normed_rel = jnp.roll(normed_rel, -at_x, axis=2)
    normed_rel = jnp.roll(normed_rel, -at_zh, axis=3)

    def contract(lhs, piece):
        return lax.dot_general(
            lhs, piece, (((1, 2, 3), (0, 1, 2)), ((), ())), preferred_element_type=jnp.float32
        )

    def fold_qk(acc, new):
        for dy, lo, hi, piece in new:
            term = contract(normed_rel[:, dy, lo:hi], piece)
            acc = term if acc is None else acc + term
        return acc

    def fold_v(acc, new):
        for dx, lo, hi, piece in new:
            term = contract(normed_rel[:, lo:hi, dx], piece[..., :v_cols])
            acc = term if acc is None else acc + term
        return acc

    packed = jnp.concatenate([w_query, key_weight, value_weight, w_out.T], axis=1)
    by_zh = stacked_ring(packed, "zh", nz, 0)
    split = q_cols + k_cols
    half_a = by_zh[:, :, :split]
    half_b = by_zh[:, :, split:]
    a_x = stacked_ring(half_a, "x", nx, 0)
    b_y = stacked_ring(half_b, "y", ny, 0)
    _, qk = ring_pieces(a_x, "y", ny, 0, fold_qk, None)
    b_pieces, projected_values = ring_pieces(b_y, "x", nx, 0, fold_v, None)
    queries_raw = qk[:, :q_cols]
    unrotated_keys = qk[:, q_cols:]
    own_places = lax.dynamic_slice_in_dim(positions, seq_at * tok_rows, tok_rows, 0)
    reach = (LOOKBACK_SPAN - 2) // tok_rows + 1

    def attend(query_matrix, stacked, key_places, valid):
        key_matrix = stacked[0].reshape(-1, local_kv, head_dim)
        value_matrix = stacked[1].reshape(-1, local_kv, head_dim)
        scores = (
            jnp.einsum(
                "qkgd,skd->kgqs", query_matrix, key_matrix, preferred_element_type=jnp.float32
            )
            * score_scale
        )
        distance = own_places[:, None] - key_places[None, :]
        allowed = valid[None, :] & (distance >= 0) & (distance < LOOKBACK_SPAN)
        weights = jnp.where(allowed[None, None], jnp.exp(scores), jnp.zeros_like(scores))
        total = jnp.sum(weights, axis=-1)
        summed = jnp.einsum(
            "kgqs,skd->qkgd",
            weights.astype(jnp.bfloat16),
            value_matrix,
            preferred_element_type=jnp.float32,
        )
        return (total, summed)

    key_matrix = rotary(
        norm_scale(unrotated_keys.reshape(tok_rows, local_kv, head_dim), key_gain), own_places
    )
    stacked = jnp.stack(
        [key_matrix.reshape(tok_rows, local_kv * head_dim), projected_values]
    ).astype(jnp.bfloat16)
    pieces = []
    for distance in range(reach, 0, -1):
        pieces.append(from_behind(stacked, SEQ, n_seq, distance))
    halo = jnp.concatenate(pieces, axis=1)
    query_matrix = rotary(
        norm_scale(queries_raw.reshape(tok_rows, local_kv * query_group, head_dim), query_gain),
        own_places,
    )
    query_matrix = query_matrix.astype(jnp.bfloat16).reshape(
        tok_rows, local_kv, query_group, head_dim
    )
    inner_total, inner_sum = attend(
        query_matrix, stacked, own_places, jnp.ones((tok_rows,), jnp.bool_)
    )
    span = halo.shape[1]
    padded_places = jnp.concatenate([jnp.zeros((span,), jnp.int32), positions])
    halo_places = lax.dynamic_slice_in_dim(padded_places, seq_at * tok_rows, span, 0)
    halo_valid = seq_at * tok_rows - span + jnp.arange(span, dtype=jnp.int32) >= 0
    outer_total, outer_sum = attend(query_matrix, halo, halo_places, halo_valid)
    total = jnp.transpose(inner_total + outer_total, (2, 0, 1))
    merged = (inner_sum + outer_sum) / total[..., None]
    attended = merged.astype(jnp.bfloat16).reshape(tok_rows, local_kv * query_group * head_dim)
    out_rel = jnp.zeros((tok_rows, ny, nx, nz, shard_rows), jnp.bfloat16)
    for dx, lo, hi, piece in b_pieces:
        cols = lax.dot_general(
            attended,
            piece[..., v_cols:],
            (((1,), (3,)), ((), ())),
            preferred_element_type=jnp.float32,
        )
        out_rel = out_rel.at[:, lo:hi, dx].set(cols.astype(jnp.bfloat16))
    out_abs = jnp.roll(out_rel, at_y, axis=1)
    out_abs = jnp.roll(out_abs, at_x, axis=2)
    out_abs = jnp.roll(out_abs, at_zh, axis=3)
    partial_out = out_abs.transpose(0, 3, 1, 2, 4).reshape(tok_rows, n_seq * shard_rows)
    summed_cols = lax.psum_scatter(
        partial_out, TP, scatter_dimension=1, tiled=True
    ).astype(jnp.float32)
    full_width = post_gain.shape[0]
    squares = lax.psum(jnp.sum(summed_cols * summed_cols, axis=1), TP)
    inverse_rms = lax.rsqrt(squares / full_width + epsilon)
    gain_part = lax.dynamic_slice_in_dim(
        post_gain, tp_at * summed_cols.shape[1], summed_cols.shape[1], 0
    )
    return (residual.astype(jnp.float32) + summed_cols * inverse_rms[:, None] * gain_part).astype(
        jnp.bfloat16
    )


def solution(mesh):
    seq_n, tp_n = mesh.devices.shape
    shape = tuple(n for _, n in SEQ_PARTS) + tuple(n for _, n in TP_PARTS)
    assert int(np.prod(shape[:3])) == seq_n and int(np.prod(shape[3:])) == tp_n
    fine = Mesh(mesh.devices.reshape(shape), SEQ + TP)
    blocked = P(SEQ, TP)
    in_specs = (
        blocked,
        P(),
        blocked,
        blocked,
        blocked,
        P(),
        P(),
        P(TP, SEQ),
        P(),
        P(),
    )
    return jax.shard_map(local, mesh=fine, in_specs=in_specs, out_specs=blocked, check_vma=False)
```

```python
import jax
import jax.numpy as jnp
import numpy as np
from jax import lax
from jax.sharding import Mesh
from jax.sharding import PartitionSpec as P

LOOKBACK_SPAN = 1024

SEQ_PARTS = (("zh", 2), ("y", 8), ("x", 4))
TP_PARTS = (("zl", 4), ("c", 2))
SEQ = tuple(name for name, _ in SEQ_PARTS)
TP = tuple(name for name, _ in TP_PARTS)

epsilon = 1e-06
score_scale = 168.0 ** (-0.5)
rotary_base = 10000.0


def from_behind(block, axis, n, distance):
    route = [(i - distance, i) for i in range(n) if i - distance >= 0]
    return lax.ppermute(block, axis, route)


def ring(block, axis, n, split_axis):
    if n == 1:
        return [block]
    fwd = [(i, (i + 1) % n) for i in range(n)]
    bwd = [(i, (i - 1) % n) for i in range(n)]
    if n == 2:
        return [block, lax.ppermute(block, axis, fwd)]
    out = [None] * n
    out[0] = block
    left, right = block, block
    for d in range(1, (n + 1) // 2):
        left = lax.ppermute(left, axis, fwd)
        right = lax.ppermute(right, axis, bwd)
        out[n - d] = left
        out[d] = right
    if n % 2 == 0:
        k = block.shape[split_axis] // 2
        top = lax.ppermute(lax.slice_in_dim(left, 0, k, axis=split_axis), axis, fwd)
        bottom = lax.ppermute(lax.slice_in_dim(right, k, None, axis=split_axis), axis, bwd)
        out[n // 2] = (top, bottom)
    return out


def stacked_ring(block, axis, n, split_axis):
    parts = ring(block, axis, n, split_axis)
    whole = [jnp.concatenate(p, axis=split_axis) if isinstance(p, tuple) else p for p in parts]
    return jnp.stack(whole, axis=0)


def ring_pieces(block, axis, n, split_axis, fold=None, acc=None):
    fwd = [(i, (i + 1) % n) for i in range(n)]
    bwd = [(i, (i - 1) % n) for i in range(n)]
    full = block.shape[split_axis]
    pieces = []

    def take(new):
        nonlocal acc
        pieces.extend(new)
        if fold is not None:
            acc = fold(acc, new)

    take([(0, 0, full, block)])
    left, right = block, block
    for d in range(1, (n + 1) // 2):
        if d > 1 and fold is not None:
            left, right, acc = lax.optimization_barrier((left, right, acc))
        left = lax.ppermute(left, axis, fwd)
        right = lax.ppermute(right, axis, bwd)
        take([(n - d, 0, full, left), (d, 0, full, right)])
    if n % 2 == 0:
        if fold is not None:
            left, right, acc = lax.optimization_barrier((left, right, acc))
        k = full // 2
        top = lax.ppermute(lax.slice_in_dim(left, 0, k, axis=split_axis), axis, fwd)
        bottom = lax.ppermute(lax.slice_in_dim(right, k, None, axis=split_axis), axis, bwd)
        take([(n // 2, 0, k, top), (n // 2, k, full, bottom)])
    return pieces, acc


def reduce_scatter_tp(partial, n_chip):
    rows = partial.shape[0]
    block_cols = partial.shape[1] // (2 * n_chip)
    at_c = lax.axis_index("c")
    at_z = lax.axis_index("zl")
    blocks = partial.reshape(rows, n_chip, 2, block_cols)
    keep = lax.dynamic_index_in_dim(blocks, at_c, axis=2, keepdims=False)
    give = lax.dynamic_index_in_dim(blocks, 1 - at_c, axis=2, keepdims=False)
    got = lax.ppermute(give, "c", [(0, 1), (1, 0)])
    chip_sum = keep.astype(jnp.float32) + got.astype(jnp.float32)
    total = lax.dynamic_index_in_dim(chip_sum, at_z, axis=1, keepdims=False)
    for d in range(1, n_chip):
        for sign in (1, -1):
            route = [(i, i + sign * d) for i in range(n_chip) if 0 <= i + sign * d < n_chip]
            target = jnp.clip(at_z + sign * d, 0, n_chip - 1)
            block = lax.dynamic_index_in_dim(chip_sum, target, axis=1, keepdims=False)
            total = total + lax.ppermute(block.astype(jnp.bfloat16), "zl", route).astype(jnp.float32)
    return total


def norm_scale(value_matrix, gain):
    mean_square = jnp.mean(value_matrix * value_matrix, axis=-1, keepdims=True)
    return value_matrix * lax.rsqrt(mean_square + epsilon) * gain


def rotary(value_matrix, places):
    half_dim = value_matrix.shape[-1] // 2
    inverse = rotary_base ** (-jnp.arange(half_dim, dtype=jnp.float32) / half_dim)
    angles = places.astype(jnp.float32)[:, None] * inverse[None, :]
    cosine = jnp.cos(angles)[:, None, :]
    sine = jnp.sin(angles)[:, None, :]
    first = value_matrix[..., :half_dim]
    second = value_matrix[..., half_dim:]
    return jnp.concatenate(
        [first * cosine - second * sine, second * cosine + first * sine], axis=-1
    )


def local(
    residual,
    input_gain,
    w_query,
    key_weight,
    value_weight,
    query_gain,
    key_gain,
    w_out,
    post_gain,
    positions,
):
    sizes = dict(SEQ_PARTS)
    n_seq = int(np.prod([n for _, n in SEQ_PARTS]))
    tok_rows = residual.shape[0]
    seq_at = lax.axis_index(SEQ)
    tp_at = lax.axis_index(TP)
    head_dim = query_gain.shape[0]
    local_kv = key_weight.shape[1] // head_dim
    query_group = w_query.shape[1] // key_weight.shape[1]
    q_cols = w_query.shape[1]
    k_cols = key_weight.shape[1]
    v_cols = value_weight.shape[1]
    shard_rows = w_query.shape[0]

    nz, ny, nx = sizes["zh"], sizes["y"], sizes["x"]
    gathered = lax.all_gather(residual, TP, axis=1, tiled=True)
    normalized_input = norm_scale(gathered.astype(jnp.float32), input_gain).astype(jnp.bfloat16)
    at_zh, at_y, at_x = (lax.axis_index(name) for name in SEQ)
    normed_rel = normalized_input.reshape(tok_rows, nz, ny, nx, shard_rows).transpose(0, 2, 3, 1, 4)
    normed_rel = jnp.roll(normed_rel, -at_y, axis=1)
    normed_rel = jnp.roll(normed_rel, -at_x, axis=2)
    normed_rel = jnp.roll(normed_rel, -at_zh, axis=3)

    def contract(lhs, piece):
        return lax.dot_general(
            lhs, piece, (((1, 2, 3), (0, 1, 2)), ((), ())), preferred_element_type=jnp.float32
        )

    def fold_qk(acc, new):
        for dy, lo, hi, piece in new:
            term = contract(normed_rel[:, dy, lo:hi], piece)
            acc = term if acc is None else acc + term
        return acc

    def fold_v(acc, new):
        for dx, lo, hi, piece in new:
            term = contract(normed_rel[:, lo:hi, dx], piece[..., :v_cols])
            acc = term if acc is None else acc + term
        return acc

    packed = jnp.concatenate([w_query, key_weight, value_weight, w_out.T], axis=1)
    by_zh = stacked_ring(packed, "zh", nz, 0)
    split = q_cols + k_cols
    half_a = by_zh[:, :, :split]
    half_b = by_zh[:, :, split:]
    a_x = stacked_ring(half_a, "x", nx, 0)
    b_y = stacked_ring(half_b, "y", ny, 0)
    _, qk = ring_pieces(a_x, "y", ny, 0, fold_qk, None)
    b_pieces, projected_values = ring_pieces(b_y, "x", nx, 0, fold_v, None)
    queries_raw = qk[:, :q_cols]
    unrotated_keys = qk[:, q_cols:]
    own_places = lax.dynamic_slice_in_dim(positions, seq_at * tok_rows, tok_rows, 0)
    reach = (LOOKBACK_SPAN - 2) // tok_rows + 1

    def attend(query_matrix, stacked, key_places, valid):
        key_matrix = stacked[0].reshape(-1, local_kv, head_dim)
        value_matrix = stacked[1].reshape(-1, local_kv, head_dim)
        scores = (
            jnp.einsum(
                "qkgd,skd->kgqs", query_matrix, key_matrix, preferred_element_type=jnp.float32
            )
            * score_scale
        )
        distance = own_places[:, None] - key_places[None, :]
        allowed = valid[None, :] & (distance >= 0) & (distance < LOOKBACK_SPAN)
        weights = jnp.where(allowed[None, None], jnp.exp(scores), jnp.zeros_like(scores))
        total = jnp.sum(weights, axis=-1)
        summed = jnp.einsum(
            "kgqs,skd->qkgd",
            weights.astype(jnp.bfloat16),
            value_matrix,
            preferred_element_type=jnp.float32,
        )
        return (total, summed)

    key_matrix = rotary(
        norm_scale(unrotated_keys.reshape(tok_rows, local_kv, head_dim), key_gain), own_places
    )
    stacked = jnp.stack(
        [key_matrix.reshape(tok_rows, local_kv * head_dim), projected_values]
    ).astype(jnp.bfloat16)
    pieces = []
    for distance in range(reach, 0, -1):
        pieces.append(from_behind(stacked, SEQ, n_seq, distance))
    halo = jnp.concatenate(pieces, axis=1)
    query_matrix = rotary(
        norm_scale(queries_raw.reshape(tok_rows, local_kv * query_group, head_dim), query_gain),
        own_places,
    )
    query_matrix = query_matrix.astype(jnp.bfloat16).reshape(
        tok_rows, local_kv, query_group, head_dim
    )
    inner_total, inner_sum = attend(
        query_matrix, stacked, own_places, jnp.ones((tok_rows,), jnp.bool_)
    )
    span = halo.shape[1]
    padded_places = jnp.concatenate([jnp.zeros((span,), jnp.int32), positions])
    halo_places = lax.dynamic_slice_in_dim(padded_places, seq_at * tok_rows, span, 0)
    halo_valid = seq_at * tok_rows - span + jnp.arange(span, dtype=jnp.int32) >= 0
    outer_total, outer_sum = attend(query_matrix, halo, halo_places, halo_valid)
    total = jnp.transpose(inner_total + outer_total, (2, 0, 1))
    merged = (inner_sum + outer_sum) / total[..., None]
    attended = merged.astype(jnp.bfloat16).reshape(tok_rows, local_kv * query_group * head_dim)
    out_rel = jnp.zeros((tok_rows, ny, nx, nz, shard_rows), jnp.bfloat16)
    for dx, lo, hi, piece in b_pieces:
        cols = lax.dot_general(
            attended,
            piece[..., v_cols:],
            (((1,), (3,)), ((), ())),
            preferred_element_type=jnp.float32,
        )
        out_rel = out_rel.at[:, lo:hi, dx].set(cols.astype(jnp.bfloat16))
    out_abs = jnp.roll(out_rel, at_y, axis=1)
    out_abs = jnp.roll(out_abs, at_x, axis=2)
    out_abs = jnp.roll(out_abs, at_zh, axis=3)
    partial_out = out_abs.transpose(0, 3, 1, 2, 4).reshape(tok_rows, n_seq * shard_rows)
    summed_cols = reduce_scatter_tp(partial_out, dict(TP_PARTS)["zl"])
    full_width = post_gain.shape[0]
    squares = lax.psum(jnp.sum(summed_cols * summed_cols, axis=1), TP)
    inverse_rms = lax.rsqrt(squares / full_width + epsilon)
    gain_part = lax.dynamic_slice_in_dim(
        post_gain, tp_at * summed_cols.shape[1], summed_cols.shape[1], 0
    )
    return (residual.astype(jnp.float32) + summed_cols * inverse_rms[:, None] * gain_part).astype(
        jnp.bfloat16
    )


def solution(mesh):
    seq_n, tp_n = mesh.devices.shape
    shape = tuple(n for _, n in SEQ_PARTS) + tuple(n for _, n in TP_PARTS)
    assert int(np.prod(shape[:3])) == seq_n and int(np.prod(shape[3:])) == tp_n
    fine = Mesh(mesh.devices.reshape(shape), SEQ + TP)
    blocked = P(SEQ, TP)
    in_specs = (
        blocked,
        P(),
        blocked,
        blocked,
        blocked,
        P(),
        P(),
        P(TP, SEQ),
        P(),
        P(),
    )
    return jax.shard_map(local, mesh=fine, in_specs=in_specs, out_specs=blocked, check_vma=False)
```

```python
import jax
import jax.numpy as jnp
import numpy as np
from jax import lax
from jax.sharding import Mesh
from jax.sharding import PartitionSpec as P

LOOKBACK_SPAN = 1024

SEQ_PARTS = (("zh", 2), ("y", 8), ("x", 4))
TP_PARTS = (("zl", 4), ("c", 2))
SEQ = tuple(name for name, _ in SEQ_PARTS)
TP = tuple(name for name, _ in TP_PARTS)

epsilon = 1e-06
score_scale = 168.0 ** (-0.5)
rotary_base = 10000.0


def from_behind(block, axis, n, distance):
    route = [(i - distance, i) for i in range(n) if i - distance >= 0]
    return lax.ppermute(block, axis, route)


def ring(block, axis, n, split_axis):
    if n == 1:
        return [block]
    fwd = [(i, (i + 1) % n) for i in range(n)]
    bwd = [(i, (i - 1) % n) for i in range(n)]
    if n == 2:
        return [block, lax.ppermute(block, axis, fwd)]
    out = [None] * n
    out[0] = block
    left, right = block, block
    for d in range(1, (n + 1) // 2):
        left = lax.ppermute(left, axis, fwd)
        right = lax.ppermute(right, axis, bwd)
        out[n - d] = left
        out[d] = right
    if n % 2 == 0:
        k = block.shape[split_axis] // 2
        top = lax.ppermute(lax.slice_in_dim(left, 0, k, axis=split_axis), axis, fwd)
        bottom = lax.ppermute(lax.slice_in_dim(right, k, None, axis=split_axis), axis, bwd)
        out[n // 2] = (top, bottom)
    return out


def stacked_ring(block, axis, n, split_axis):
    parts = ring(block, axis, n, split_axis)
    whole = [jnp.concatenate(p, axis=split_axis) if isinstance(p, tuple) else p for p in parts]
    return jnp.stack(whole, axis=0)


def ring_pieces(block, axis, n, split_axis, fold=None, acc=None):
    fwd = [(i, (i + 1) % n) for i in range(n)]
    bwd = [(i, (i - 1) % n) for i in range(n)]
    full = block.shape[split_axis]
    pieces = []

    def take(new):
        nonlocal acc
        pieces.extend(new)
        if fold is not None:
            acc = fold(acc, new)

    take([(0, 0, full, block)])
    left, right = block, block
    for d in range(1, (n + 1) // 2):
        if d > 1 and fold is not None:
            left, right, acc = lax.optimization_barrier((left, right, acc))
        left = lax.ppermute(left, axis, fwd)
        right = lax.ppermute(right, axis, bwd)
        take([(n - d, 0, full, left), (d, 0, full, right)])
    if n % 2 == 0:
        if fold is not None:
            left, right, acc = lax.optimization_barrier((left, right, acc))
        k = full // 2
        top = lax.ppermute(lax.slice_in_dim(left, 0, k, axis=split_axis), axis, fwd)
        bottom = lax.ppermute(lax.slice_in_dim(right, k, None, axis=split_axis), axis, bwd)
        take([(n // 2, 0, k, top), (n // 2, k, full, bottom)])
    return pieces, acc


def reduce_scatter_tp(partial, n_chip):
    rows = partial.shape[0]
    block_cols = partial.shape[1] // (2 * n_chip)
    at_c = lax.axis_index("c")
    at_z = lax.axis_index("zl")
    blocks = partial.reshape(rows, n_chip, 2, block_cols)
    keep = lax.dynamic_index_in_dim(blocks, at_c, axis=2, keepdims=False)
    give = lax.dynamic_index_in_dim(blocks, 1 - at_c, axis=2, keepdims=False)
    got = lax.ppermute(give, "c", [(0, 1), (1, 0)])
    chip_sum = keep.astype(jnp.float32) + got.astype(jnp.float32)
    total = lax.dynamic_index_in_dim(chip_sum, at_z, axis=1, keepdims=False)
    for d in range(1, n_chip):
        for sign in (1, -1):
            route = [(i, i + sign * d) for i in range(n_chip) if 0 <= i + sign * d < n_chip]
            target = jnp.clip(at_z + sign * d, 0, n_chip - 1)
            block = lax.dynamic_index_in_dim(chip_sum, target, axis=1, keepdims=False)
            total = total + lax.ppermute(block.astype(jnp.bfloat16), "zl", route).astype(jnp.float32)
    return total


def norm_scale(value_matrix, gain):
    mean_square = jnp.mean(value_matrix * value_matrix, axis=-1, keepdims=True)
    return value_matrix * lax.rsqrt(mean_square + epsilon) * gain


def rotary(value_matrix, places):
    half_dim = value_matrix.shape[-1] // 2
    inverse = rotary_base ** (-jnp.arange(half_dim, dtype=jnp.float32) / half_dim)
    angles = places.astype(jnp.float32)[:, None] * inverse[None, :]
    cosine = jnp.cos(angles)[:, None, :]
    sine = jnp.sin(angles)[:, None, :]
    first = value_matrix[..., :half_dim]
    second = value_matrix[..., half_dim:]
    return jnp.concatenate(
        [first * cosine - second * sine, second * cosine + first * sine], axis=-1
    )


def local(
    residual,
    input_gain,
    w_query,
    key_weight,
    value_weight,
    query_gain,
    key_gain,
    w_out,
    post_gain,
    positions,
):
    sizes = dict(SEQ_PARTS)
    n_seq = int(np.prod([n for _, n in SEQ_PARTS]))
    tok_rows = residual.shape[0]
    seq_at = lax.axis_index(SEQ)
    tp_at = lax.axis_index(TP)
    head_dim = query_gain.shape[0]
    local_kv = key_weight.shape[1] // head_dim
    query_group = w_query.shape[1] // key_weight.shape[1]
    q_cols = w_query.shape[1]
    k_cols = key_weight.shape[1]
    v_cols = value_weight.shape[1]
    shard_rows = w_query.shape[0]

    nz, ny, nx = sizes["zh"], sizes["y"], sizes["x"]
    gathered = lax.all_gather(residual, TP, axis=1, tiled=True)
    normalized_input = norm_scale(gathered.astype(jnp.float32), input_gain).astype(jnp.bfloat16)
    at_zh, at_y, at_x = (lax.axis_index(name) for name in SEQ)
    normed_rel = normalized_input.reshape(tok_rows, nz, ny, nx, shard_rows).transpose(0, 2, 3, 1, 4)
    normed_rel = jnp.roll(normed_rel, -at_y, axis=1)
    normed_rel = jnp.roll(normed_rel, -at_x, axis=2)
    normed_rel = jnp.roll(normed_rel, -at_zh, axis=3)

    def contract(lhs, piece):
        return lax.dot_general(
            lhs, piece, (((1, 2, 3), (0, 1, 2)), ((), ())), preferred_element_type=jnp.float32
        )

    def fold_qk(acc, new):
        for dy, lo, hi, piece in new:
            term = contract(normed_rel[:, dy, lo:hi], piece)
            acc = term if acc is None else acc + term
        return acc

    def fold_kv(acc, new):
        for dx, lo, hi, piece in new:
            term = contract(normed_rel[:, lo:hi, dx], piece)
            acc = term if acc is None else acc + term
        return acc

    packed = jnp.concatenate([w_query, key_weight, value_weight], axis=1)
    by_zh = stacked_ring(packed, "zh", nz, 0)
    split = q_cols
    half_a = by_zh[:, :, :split]
    half_b = by_zh[:, :, split:]
    a_x = stacked_ring(half_a, "x", nx, 0)
    b_y = stacked_ring(half_b, "y", ny, 0)
    _, queries_raw = ring_pieces(a_x, "y", ny, 0, fold_qk, None)
    _, kv = ring_pieces(b_y, "x", nx, 0, fold_kv, None)
    unrotated_keys = kv[:, :k_cols]
    projected_values = kv[:, k_cols:]
    _, w_out_after = lax.optimization_barrier((gathered, w_out))
    w_out_full = lax.all_gather(w_out_after, SEQ, axis=1, tiled=True)
    own_places = lax.dynamic_slice_in_dim(positions, seq_at * tok_rows, tok_rows, 0)
    reach = (LOOKBACK_SPAN - 2) // tok_rows + 1

    def attend(query_matrix, stacked, key_places, valid):
        key_matrix = stacked[0].reshape(-1, local_kv, head_dim)
        value_matrix = stacked[1].reshape(-1, local_kv, head_dim)
        scores = (
            jnp.einsum(
                "qkgd,skd->kgqs", query_matrix, key_matrix, preferred_element_type=jnp.float32
            )
            * score_scale
        )
        distance = own_places[:, None] - key_places[None, :]
        allowed = valid[None, :] & (distance >= 0) & (distance < LOOKBACK_SPAN)
        weights = jnp.where(allowed[None, None], jnp.exp(scores), jnp.zeros_like(scores))
        total = jnp.sum(weights, axis=-1)
        summed = jnp.einsum(
            "kgqs,skd->qkgd",
            weights.astype(jnp.bfloat16),
            value_matrix,
            preferred_element_type=jnp.float32,
        )
        return (total, summed)

    key_matrix = rotary(
        norm_scale(unrotated_keys.reshape(tok_rows, local_kv, head_dim), key_gain), own_places
    )
    stacked = jnp.stack(
        [key_matrix.reshape(tok_rows, local_kv * head_dim), projected_values]
    ).astype(jnp.bfloat16)
    pieces = []
    for distance in range(reach, 0, -1):
        pieces.append(from_behind(stacked, SEQ, n_seq, distance))
    halo = jnp.concatenate(pieces, axis=1)
    query_matrix = rotary(
        norm_scale(queries_raw.reshape(tok_rows, local_kv * query_group, head_dim), query_gain),
        own_places,
    )
    query_matrix = query_matrix.astype(jnp.bfloat16).reshape(
        tok_rows, local_kv, query_group, head_dim
    )
    inner_total, inner_sum = attend(
        query_matrix, stacked, own_places, jnp.ones((tok_rows,), jnp.bool_)
    )
    span = halo.shape[1]
    padded_places = jnp.concatenate([jnp.zeros((span,), jnp.int32), positions])
    halo_places = lax.dynamic_slice_in_dim(padded_places, seq_at * tok_rows, span, 0)
    halo_valid = seq_at * tok_rows - span + jnp.arange(span, dtype=jnp.int32) >= 0
    outer_total, outer_sum = attend(query_matrix, halo, halo_places, halo_valid)
    total = jnp.transpose(inner_total + outer_total, (2, 0, 1))
    merged = (inner_sum + outer_sum) / total[..., None]
    attended = merged.astype(jnp.bfloat16).reshape(tok_rows, local_kv * query_group * head_dim)
    partial_out = jnp.dot(attended, w_out_full, preferred_element_type=jnp.float32).astype(
        jnp.bfloat16
    )
    summed_cols = reduce_scatter_tp(partial_out, dict(TP_PARTS)["zl"])
    full_width = post_gain.shape[0]
    squares = lax.psum(jnp.sum(summed_cols * summed_cols, axis=1), TP)
    inverse_rms = lax.rsqrt(squares / full_width + epsilon)
    gain_part = lax.dynamic_slice_in_dim(
        post_gain, tp_at * summed_cols.shape[1], summed_cols.shape[1], 0
    )
    return (residual.astype(jnp.float32) + summed_cols * inverse_rms[:, None] * gain_part).astype(
        jnp.bfloat16
    )


def solution(mesh):
    seq_n, tp_n = mesh.devices.shape
    shape = tuple(n for _, n in SEQ_PARTS) + tuple(n for _, n in TP_PARTS)
    assert int(np.prod(shape[:3])) == seq_n and int(np.prod(shape[3:])) == tp_n
    fine = Mesh(mesh.devices.reshape(shape), SEQ + TP)
    blocked = P(SEQ, TP)
    in_specs = (
        blocked,
        P(),
        blocked,
        blocked,
        blocked,
        P(),
        P(),
        P(TP, SEQ),
        P(),
        P(),
    )
    return jax.shard_map(local, mesh=fine, in_specs=in_specs, out_specs=blocked, check_vma=False)
```

```python
import jax
import jax.numpy as jnp
import numpy as np
from jax import lax
from jax.sharding import Mesh
from jax.sharding import PartitionSpec as P

LOOKBACK_SPAN = 1024

SEQ_PARTS = (("zh", 2), ("y", 8), ("x", 4))
TP_PARTS = (("zl", 4), ("c", 2))
SEQ = tuple(name for name, _ in SEQ_PARTS)
TP = tuple(name for name, _ in TP_PARTS)

epsilon = 1e-06
score_scale = 168.0 ** (-0.5)
rotary_base = 10000.0


def from_behind(block, axis, n, distance):
    route = [(i - distance, i) for i in range(n) if i - distance >= 0]
    return lax.ppermute(block, axis, route)


def ring(block, axis, n, split_axis):
    if n == 1:
        return [block]
    fwd = [(i, (i + 1) % n) for i in range(n)]
    bwd = [(i, (i - 1) % n) for i in range(n)]
    if n == 2:
        return [block, lax.ppermute(block, axis, fwd)]
    out = [None] * n
    out[0] = block
    left, right = block, block
    for d in range(1, (n + 1) // 2):
        left = lax.ppermute(left, axis, fwd)
        right = lax.ppermute(right, axis, bwd)
        out[n - d] = left
        out[d] = right
    if n % 2 == 0:
        k = block.shape[split_axis] // 2
        top = lax.ppermute(lax.slice_in_dim(left, 0, k, axis=split_axis), axis, fwd)
        bottom = lax.ppermute(lax.slice_in_dim(right, k, None, axis=split_axis), axis, bwd)
        out[n // 2] = (top, bottom)
    return out


def stacked_ring(block, axis, n, split_axis):
    parts = ring(block, axis, n, split_axis)
    whole = [jnp.concatenate(p, axis=split_axis) if isinstance(p, tuple) else p for p in parts]
    return jnp.stack(whole, axis=0)


def stacked_direct(block, axis, n):
    parts = [block] + [
        lax.ppermute(block, axis, [(j, (j - d) % n) for j in range(n)]) for d in range(1, n)
    ]
    return jnp.stack(parts, axis=0)


def ring_pieces(block, axis, n, split_axis, fold=None, acc=None):
    fwd = [(i, (i + 1) % n) for i in range(n)]
    bwd = [(i, (i - 1) % n) for i in range(n)]
    full = block.shape[split_axis]
    pieces = []

    def take(new):
        nonlocal acc
        pieces.extend(new)
        if fold is not None:
            acc = fold(acc, new)

    take([(0, 0, full, block)])
    left, right = block, block
    for d in range(1, (n + 1) // 2):
        if d > 1 and fold is not None:
            left, right, acc = lax.optimization_barrier((left, right, acc))
        left = lax.ppermute(left, axis, fwd)
        right = lax.ppermute(right, axis, bwd)
        take([(n - d, 0, full, left), (d, 0, full, right)])
    if n % 2 == 0:
        if fold is not None:
            left, right, acc = lax.optimization_barrier((left, right, acc))
        k = full // 2
        top = lax.ppermute(lax.slice_in_dim(left, 0, k, axis=split_axis), axis, fwd)
        bottom = lax.ppermute(lax.slice_in_dim(right, k, None, axis=split_axis), axis, bwd)
        take([(n // 2, 0, k, top), (n // 2, k, full, bottom)])
    return pieces, acc


def reduce_scatter_tp(partial, n_chip):
    rows = partial.shape[0]
    block_cols = partial.shape[1] // (2 * n_chip)
    at_c = lax.axis_index("c")
    at_z = lax.axis_index("zl")
    blocks = partial.reshape(rows, n_chip, 2, block_cols)
    keep = lax.dynamic_index_in_dim(blocks, at_c, axis=2, keepdims=False)
    give = lax.dynamic_index_in_dim(blocks, 1 - at_c, axis=2, keepdims=False)
    got = lax.ppermute(give, "c", [(0, 1), (1, 0)])
    chip_sum = keep.astype(jnp.float32) + got.astype(jnp.float32)
    total = lax.dynamic_index_in_dim(chip_sum, at_z, axis=1, keepdims=False)
    for d in range(1, n_chip):
        for sign in (1, -1):
            route = [(i, i + sign * d) for i in range(n_chip) if 0 <= i + sign * d < n_chip]
            target = jnp.clip(at_z + sign * d, 0, n_chip - 1)
            block = lax.dynamic_index_in_dim(chip_sum, target, axis=1, keepdims=False)
            total = total + lax.ppermute(block.astype(jnp.bfloat16), "zl", route).astype(jnp.float32)
    return total


def norm_scale(value_matrix, gain):
    mean_square = jnp.mean(value_matrix * value_matrix, axis=-1, keepdims=True)
    return value_matrix * lax.rsqrt(mean_square + epsilon) * gain


def rotary(value_matrix, places):
    half_dim = value_matrix.shape[-1] // 2
    inverse = rotary_base ** (-jnp.arange(half_dim, dtype=jnp.float32) / half_dim)
    angles = places.astype(jnp.float32)[:, None] * inverse[None, :]
    cosine = jnp.cos(angles)[:, None, :]
    sine = jnp.sin(angles)[:, None, :]
    first = value_matrix[..., :half_dim]
    second = value_matrix[..., half_dim:]
    return jnp.concatenate(
        [first * cosine - second * sine, second * cosine + first * sine], axis=-1
    )


def local(
    residual,
    input_gain,
    w_query,
    key_weight,
    value_weight,
    query_gain,
    key_gain,
    w_out,
    post_gain,
    positions,
):
    sizes = dict(SEQ_PARTS)
    n_seq = int(np.prod([n for _, n in SEQ_PARTS]))
    tok_rows = residual.shape[0]
    seq_at = lax.axis_index(SEQ)
    tp_at = lax.axis_index(TP)
    head_dim = query_gain.shape[0]
    local_kv = key_weight.shape[1] // head_dim
    query_group = w_query.shape[1] // key_weight.shape[1]
    q_cols = w_query.shape[1]
    k_cols = key_weight.shape[1]
    v_cols = value_weight.shape[1]
    shard_rows = w_query.shape[0]

    nz, ny, nx = sizes["zh"], sizes["y"], sizes["x"]
    gathered = lax.all_gather(residual, TP, axis=1, tiled=True)
    normalized_input = norm_scale(gathered.astype(jnp.float32), input_gain).astype(jnp.bfloat16)
    at_zh, at_y, at_x = (lax.axis_index(name) for name in SEQ)
    normed_rel = normalized_input.reshape(tok_rows, nz, ny, nx, shard_rows).transpose(0, 2, 3, 1, 4)
    normed_rel = jnp.roll(normed_rel, -at_y, axis=1)
    normed_rel = jnp.roll(normed_rel, -at_x, axis=2)
    normed_rel = jnp.roll(normed_rel, -at_zh, axis=3)

    def contract(lhs, piece):
        return lax.dot_general(
            lhs, piece, (((1, 2, 3), (0, 1, 2)), ((), ())), preferred_element_type=jnp.float32
        )

    def fold_qk(acc, new):
        for dy, lo, hi, piece in new:
            term = contract(normed_rel[:, dy, lo:hi], piece)
            acc = term if acc is None else acc + term
        return acc

    def fold_v(acc, new):
        for dx, lo, hi, piece in new:
            term = contract(normed_rel[:, lo:hi, dx], piece[..., :v_cols])
            acc = term if acc is None else acc + term
        return acc

    packed = jnp.concatenate([w_query, key_weight, value_weight, w_out.T], axis=1)
    by_zh = stacked_ring(packed, "zh", nz, 0)
    split = q_cols + k_cols
    half_a = by_zh[:, :, :split]
    half_b = by_zh[:, :, split:]
    a_x = stacked_direct(half_a, "x", nx)
    b_y = stacked_ring(half_b, "y", ny, 0)
    _, qk = ring_pieces(a_x, "y", ny, 0, fold_qk, None)
    b_pieces, projected_values = ring_pieces(b_y, "x", nx, 0, fold_v, None)
    queries_raw = qk[:, :q_cols]
    unrotated_keys = qk[:, q_cols:]
    own_places = lax.dynamic_slice_in_dim(positions, seq_at * tok_rows, tok_rows, 0)
    reach = (LOOKBACK_SPAN - 2) // tok_rows + 1

    def attend(query_matrix, stacked, key_places, valid):
        key_matrix = stacked[0].reshape(-1, local_kv, head_dim)
        value_matrix = stacked[1].reshape(-1, local_kv, head_dim)
        scores = (
            jnp.einsum(
                "qkgd,skd->kgqs", query_matrix, key_matrix, preferred_element_type=jnp.float32
            )
            * score_scale
        )
        distance = own_places[:, None] - key_places[None, :]
        allowed = valid[None, :] & (distance >= 0) & (distance < LOOKBACK_SPAN)
        weights = jnp.where(allowed[None, None], jnp.exp(scores), jnp.zeros_like(scores))
        total = jnp.sum(weights, axis=-1)
        summed = jnp.einsum(
            "kgqs,skd->qkgd",
            weights.astype(jnp.bfloat16),
            value_matrix,
            preferred_element_type=jnp.float32,
        )
        return (total, summed)

    key_matrix = rotary(
        norm_scale(unrotated_keys.reshape(tok_rows, local_kv, head_dim), key_gain), own_places
    )
    stacked = jnp.stack(
        [key_matrix.reshape(tok_rows, local_kv * head_dim), projected_values]
    ).astype(jnp.bfloat16)
    pieces = []
    for distance in range(reach, 0, -1):
        pieces.append(from_behind(stacked, SEQ, n_seq, distance))
    halo = jnp.concatenate(pieces, axis=1)
    query_matrix = rotary(
        norm_scale(queries_raw.reshape(tok_rows, local_kv * query_group, head_dim), query_gain),
        own_places,
    )
    query_matrix = query_matrix.astype(jnp.bfloat16).reshape(
        tok_rows, local_kv, query_group, head_dim
    )
    inner_total, inner_sum = attend(
        query_matrix, stacked, own_places, jnp.ones((tok_rows,), jnp.bool_)
    )
    span = halo.shape[1]
    padded_places = jnp.concatenate([jnp.zeros((span,), jnp.int32), positions])
    halo_places = lax.dynamic_slice_in_dim(padded_places, seq_at * tok_rows, span, 0)
    halo_valid = seq_at * tok_rows - span + jnp.arange(span, dtype=jnp.int32) >= 0
    outer_total, outer_sum = attend(query_matrix, halo, halo_places, halo_valid)
    total = jnp.transpose(inner_total + outer_total, (2, 0, 1))
    merged = (inner_sum + outer_sum) / total[..., None]
    attended = merged.astype(jnp.bfloat16).reshape(tok_rows, local_kv * query_group * head_dim)
    out_rel = jnp.zeros((tok_rows, ny, nx, nz, shard_rows), jnp.bfloat16)
    for dx, lo, hi, piece in b_pieces:
        cols = lax.dot_general(
            attended,
            piece[..., v_cols:],
            (((1,), (3,)), ((), ())),
            preferred_element_type=jnp.float32,
        )
        out_rel = out_rel.at[:, lo:hi, dx].set(cols.astype(jnp.bfloat16))
    out_abs = jnp.roll(out_rel, at_y, axis=1)
    out_abs = jnp.roll(out_abs, at_x, axis=2)
    out_abs = jnp.roll(out_abs, at_zh, axis=3)
    partial_out = out_abs.transpose(0, 3, 1, 2, 4).reshape(tok_rows, n_seq * shard_rows)
    summed_cols = reduce_scatter_tp(partial_out, dict(TP_PARTS)["zl"])
    full_width = post_gain.shape[0]
    squares = lax.psum(jnp.sum(summed_cols * summed_cols, axis=1), TP)
    inverse_rms = lax.rsqrt(squares / full_width + epsilon)
    gain_part = lax.dynamic_slice_in_dim(
        post_gain, tp_at * summed_cols.shape[1], summed_cols.shape[1], 0
    )
    return (residual.astype(jnp.float32) + summed_cols * inverse_rms[:, None] * gain_part).astype(
        jnp.bfloat16
    )


def solution(mesh):
    seq_n, tp_n = mesh.devices.shape
    shape = tuple(n for _, n in SEQ_PARTS) + tuple(n for _, n in TP_PARTS)
    assert int(np.prod(shape[:3])) == seq_n and int(np.prod(shape[3:])) == tp_n
    fine = Mesh(mesh.devices.reshape(shape), SEQ + TP)
    blocked = P(SEQ, TP)
    in_specs = (
        blocked,
        P(),
        blocked,
        blocked,
        blocked,
        P(),
        P(),
        P(TP, SEQ),
        P(),
        P(),
    )
    return jax.shard_map(local, mesh=fine, in_specs=in_specs, out_specs=blocked, check_vma=False)
```

```python
import jax
import jax.numpy as jnp
import numpy as np
from jax import lax
from jax.sharding import Mesh
from jax.sharding import PartitionSpec as P

LOOKBACK_SPAN = 1024

SEQ_PARTS = (("zh", 2), ("y", 8), ("x", 4))
TP_PARTS = (("zl", 4), ("c", 2))
SEQ = tuple(name for name, _ in SEQ_PARTS)
TP = tuple(name for name, _ in TP_PARTS)

epsilon = 1e-06
score_scale = 168.0 ** (-0.5)
rotary_base = 10000.0


def from_behind(block, axis, n, distance):
    route = [(i - distance, i) for i in range(n) if i - distance >= 0]
    return lax.ppermute(block, axis, route)


def ring(block, axis, n, split_axis):
    if n == 1:
        return [block]
    fwd = [(i, (i + 1) % n) for i in range(n)]
    bwd = [(i, (i - 1) % n) for i in range(n)]
    if n == 2:
        return [block, lax.ppermute(block, axis, fwd)]
    out = [None] * n
    out[0] = block
    left, right = block, block
    for d in range(1, (n + 1) // 2):
        left = lax.ppermute(left, axis, fwd)
        right = lax.ppermute(right, axis, bwd)
        out[n - d] = left
        out[d] = right
    if n % 2 == 0:
        k = block.shape[split_axis] // 2
        top = lax.ppermute(lax.slice_in_dim(left, 0, k, axis=split_axis), axis, fwd)
        bottom = lax.ppermute(lax.slice_in_dim(right, k, None, axis=split_axis), axis, bwd)
        out[n // 2] = (top, bottom)
    return out


def stacked_ring(block, axis, n, split_axis):
    parts = ring(block, axis, n, split_axis)
    whole = [jnp.concatenate(p, axis=split_axis) if isinstance(p, tuple) else p for p in parts]
    return jnp.stack(whole, axis=0)


def stacked_direct(block, axis, n):
    parts = [block] + [
        lax.ppermute(block, axis, [(j, (j - d) % n) for j in range(n)]) for d in range(1, n)
    ]
    return jnp.stack(parts, axis=0)


def ring_pieces(block, axis, n, split_axis, fold=None, acc=None):
    fwd = [(i, (i + 1) % n) for i in range(n)]
    bwd = [(i, (i - 1) % n) for i in range(n)]
    full = block.shape[split_axis]
    pieces = []

    def take(new):
        nonlocal acc
        pieces.extend(new)
        if fold is not None:
            acc = fold(acc, new)

    take([(0, 0, full, block)])
    left, right = block, block
    for d in range(1, (n + 1) // 2):
        if d > 1 and fold is not None:
            left, right, acc = lax.optimization_barrier((left, right, acc))
        left = lax.ppermute(left, axis, fwd)
        right = lax.ppermute(right, axis, bwd)
        take([(n - d, 0, full, left), (d, 0, full, right)])
    if n % 2 == 0:
        if fold is not None:
            left, right, acc = lax.optimization_barrier((left, right, acc))
        k = full // 2
        top = lax.ppermute(lax.slice_in_dim(left, 0, k, axis=split_axis), axis, fwd)
        bottom = lax.ppermute(lax.slice_in_dim(right, k, None, axis=split_axis), axis, bwd)
        take([(n // 2, 0, k, top), (n // 2, k, full, bottom)])
    return pieces, acc


def reduce_scatter_tp(partial, n_chip):
    rows = partial.shape[0]
    block_cols = partial.shape[1] // (2 * n_chip)
    at_c = lax.axis_index("c")
    at_z = lax.axis_index("zl")
    blocks = partial.reshape(rows, n_chip, 2, block_cols)
    keep = lax.dynamic_index_in_dim(blocks, at_c, axis=2, keepdims=False)
    give = lax.dynamic_index_in_dim(blocks, 1 - at_c, axis=2, keepdims=False)
    got = lax.ppermute(give, "c", [(0, 1), (1, 0)])
    chip_sum = keep.astype(jnp.float32) + got.astype(jnp.float32)
    total = lax.dynamic_index_in_dim(chip_sum, at_z, axis=1, keepdims=False)
    for d in range(1, n_chip):
        for sign in (1, -1):
            route = [(i, i + sign * d) for i in range(n_chip) if 0 <= i + sign * d < n_chip]
            target = jnp.clip(at_z + sign * d, 0, n_chip - 1)
            block = lax.dynamic_index_in_dim(chip_sum, target, axis=1, keepdims=False)
            total = total + lax.ppermute(block.astype(jnp.bfloat16), "zl", route).astype(jnp.float32)
    return total


def norm_scale(value_matrix, gain):
    mean_square = jnp.mean(value_matrix * value_matrix, axis=-1, keepdims=True)
    return value_matrix * lax.rsqrt(mean_square + epsilon) * gain


def rotary(value_matrix, places):
    half_dim = value_matrix.shape[-1] // 2
    inverse = rotary_base ** (-jnp.arange(half_dim, dtype=jnp.float32) / half_dim)
    angles = places.astype(jnp.float32)[:, None] * inverse[None, :]
    cosine = jnp.cos(angles)[:, None, :]
    sine = jnp.sin(angles)[:, None, :]
    first = value_matrix[..., :half_dim]
    second = value_matrix[..., half_dim:]
    return jnp.concatenate(
        [first * cosine - second * sine, second * cosine + first * sine], axis=-1
    )


def local(
    residual,
    input_gain,
    w_query,
    key_weight,
    value_weight,
    query_gain,
    key_gain,
    w_out,
    post_gain,
    positions,
):
    sizes = dict(SEQ_PARTS)
    n_seq = int(np.prod([n for _, n in SEQ_PARTS]))
    tok_rows = residual.shape[0]
    seq_at = lax.axis_index(SEQ)
    tp_at = lax.axis_index(TP)
    head_dim = query_gain.shape[0]
    local_kv = key_weight.shape[1] // head_dim
    query_group = w_query.shape[1] // key_weight.shape[1]
    q_cols = w_query.shape[1]
    k_cols = key_weight.shape[1]
    v_cols = value_weight.shape[1]
    shard_rows = w_query.shape[0]

    nz, ny, nx = sizes["zh"], sizes["y"], sizes["x"]
    gathered = lax.all_gather(residual, TP, axis=1, tiled=True)
    normalized_input = norm_scale(gathered.astype(jnp.float32), input_gain).astype(jnp.bfloat16)
    at_zh, at_y, at_x = (lax.axis_index(name) for name in SEQ)
    rel_y = (at_y + jnp.arange(ny)) % ny
    rel_x = (at_x + jnp.arange(nx)) % nx
    rel_z = (at_zh + jnp.arange(nz)) % nz
    rel_shard = ((rel_z[None, None, :] * ny + rel_y[:, None, None]) * nx + rel_x[None, :, None]).reshape(-1)
    normed_rel = jnp.take(
        normalized_input.reshape(tok_rows, n_seq, shard_rows), rel_shard, axis=1
    ).reshape(tok_rows, ny, nx, nz, shard_rows)

    def contract(lhs, piece):
        return lax.dot_general(
            lhs, piece, (((1, 2, 3), (0, 1, 2)), ((), ())), preferred_element_type=jnp.float32
        )

    def fold_qk(acc, new):
        for dy, lo, hi, piece in new:
            term = contract(normed_rel[:, dy, lo:hi], piece)
            acc = term if acc is None else acc + term
        return acc

    def fold_v(acc, new):
        for dx, lo, hi, piece in new:
            term = contract(normed_rel[:, lo:hi, dx], piece[..., :v_cols])
            acc = term if acc is None else acc + term
        return acc

    packed = jnp.concatenate([w_query, key_weight, value_weight, w_out.T], axis=1)
    by_zh = stacked_ring(packed, "zh", nz, 0)
    split = q_cols + k_cols
    half_a = by_zh[:, :, :split]
    half_b = by_zh[:, :, split:]
    a_x = stacked_direct(half_a, "x", nx)
    b_y = stacked_ring(half_b, "y", ny, 0)
    _, qk = ring_pieces(a_x, "y", ny, 0, fold_qk, None)
    b_pieces, projected_values = ring_pieces(b_y, "x", nx, 0, fold_v, None)
    queries_raw = qk[:, :q_cols]
    unrotated_keys = qk[:, q_cols:]
    own_places = lax.dynamic_slice_in_dim(positions, seq_at * tok_rows, tok_rows, 0)
    reach = (LOOKBACK_SPAN - 2) // tok_rows + 1

    def attend(query_matrix, stacked, key_places, valid):
        key_matrix = stacked[0].reshape(-1, local_kv, head_dim)
        value_matrix = stacked[1].reshape(-1, local_kv, head_dim)
        scores = (
            jnp.einsum(
                "qkgd,skd->kgqs", query_matrix, key_matrix, preferred_element_type=jnp.float32
            )
            * score_scale
        )
        distance = own_places[:, None] - key_places[None, :]
        allowed = valid[None, :] & (distance >= 0) & (distance < LOOKBACK_SPAN)
        weights = jnp.where(allowed[None, None], jnp.exp(scores), jnp.zeros_like(scores))
        total = jnp.sum(weights, axis=-1)
        summed = jnp.einsum(
            "kgqs,skd->qkgd",
            weights.astype(jnp.bfloat16),
            value_matrix,
            preferred_element_type=jnp.float32,
        )
        return (total, summed)

    key_matrix = rotary(
        norm_scale(unrotated_keys.reshape(tok_rows, local_kv, head_dim), key_gain), own_places
    )
    stacked = jnp.stack(
        [key_matrix.reshape(tok_rows, local_kv * head_dim), projected_values]
    ).astype(jnp.bfloat16)
    pieces = []
    for distance in range(reach, 0, -1):
        pieces.append(from_behind(stacked, SEQ, n_seq, distance))
    halo = jnp.concatenate(pieces, axis=1)
    query_matrix = rotary(
        norm_scale(queries_raw.reshape(tok_rows, local_kv * query_group, head_dim), query_gain),
        own_places,
    )
    query_matrix = query_matrix.astype(jnp.bfloat16).reshape(
        tok_rows, local_kv, query_group, head_dim
    )
    inner_total, inner_sum = attend(
        query_matrix, stacked, own_places, jnp.ones((tok_rows,), jnp.bool_)
    )
    span = halo.shape[1]
    padded_places = jnp.concatenate([jnp.zeros((span,), jnp.int32), positions])
    halo_places = lax.dynamic_slice_in_dim(padded_places, seq_at * tok_rows, span, 0)
    halo_valid = seq_at * tok_rows - span + jnp.arange(span, dtype=jnp.int32) >= 0
    outer_total, outer_sum = attend(query_matrix, halo, halo_places, halo_valid)
    total = jnp.transpose(inner_total + outer_total, (2, 0, 1))
    merged = (inner_sum + outer_sum) / total[..., None]
    attended = merged.astype(jnp.bfloat16).reshape(tok_rows, local_kv * query_group * head_dim)
    out_rel = jnp.zeros((tok_rows, ny, nx, nz, shard_rows), jnp.bfloat16)
    for dx, lo, hi, piece in b_pieces:
        cols = lax.dot_general(
            attended,
            piece[..., v_cols:],
            (((1,), (3,)), ((), ())),
            preferred_element_type=jnp.float32,
        )
        out_rel = out_rel.at[:, lo:hi, dx].set(cols.astype(jnp.bfloat16))
    abs_z, abs_y, abs_x = jnp.unravel_index(jnp.arange(n_seq), (nz, ny, nx))
    abs_rel = (((abs_y - at_y) % ny) * nx + (abs_x - at_x) % nx) * nz + (abs_z - at_zh) % nz
    partial_out = jnp.take(
        out_rel.reshape(tok_rows, n_seq, shard_rows), abs_rel, axis=1
    ).reshape(tok_rows, n_seq * shard_rows)
    summed_cols = reduce_scatter_tp(partial_out, dict(TP_PARTS)["zl"])
    full_width = post_gain.shape[0]
    squares = lax.psum(jnp.sum(summed_cols * summed_cols, axis=1), TP)
    inverse_rms = lax.rsqrt(squares / full_width + epsilon)
    gain_part = lax.dynamic_slice_in_dim(
        post_gain, tp_at * summed_cols.shape[1], summed_cols.shape[1], 0
    )
    return (residual.astype(jnp.float32) + summed_cols * inverse_rms[:, None] * gain_part).astype(
        jnp.bfloat16
    )


def solution(mesh):
    seq_n, tp_n = mesh.devices.shape
    shape = tuple(n for _, n in SEQ_PARTS) + tuple(n for _, n in TP_PARTS)
    assert int(np.prod(shape[:3])) == seq_n and int(np.prod(shape[3:])) == tp_n
    fine = Mesh(mesh.devices.reshape(shape), SEQ + TP)
    blocked = P(SEQ, TP)
    in_specs = (
        blocked,
        P(),
        blocked,
        blocked,
        blocked,
        P(),
        P(),
        P(TP, SEQ),
        P(),
        P(),
    )
    return jax.shard_map(local, mesh=fine, in_specs=in_specs, out_specs=blocked, check_vma=False)
```

```python
import jax
import jax.numpy as jnp
import numpy as np
from jax import lax
from jax.sharding import Mesh
from jax.sharding import PartitionSpec as P

LOOKBACK_SPAN = 1024

SEQ_PARTS = (("zh", 2), ("y", 8), ("x", 4))
TP_PARTS = (("zl", 4), ("c", 2))
SEQ = tuple(name for name, _ in SEQ_PARTS)
TP = tuple(name for name, _ in TP_PARTS)

epsilon = 1e-06
score_scale = 168.0 ** (-0.5)
rotary_base = 10000.0


def from_behind(block, axis, n, distance):
    route = [(i - distance, i) for i in range(n) if i - distance >= 0]
    return lax.ppermute(block, axis, route)


def ring(block, axis, n, split_axis):
    if n == 1:
        return [block]
    fwd = [(i, (i + 1) % n) for i in range(n)]
    bwd = [(i, (i - 1) % n) for i in range(n)]
    if n == 2:
        return [block, lax.ppermute(block, axis, fwd)]
    out = [None] * n
    out[0] = block
    left, right = block, block
    for d in range(1, (n + 1) // 2):
        left = lax.ppermute(left, axis, fwd)
        right = lax.ppermute(right, axis, bwd)
        out[n - d] = left
        out[d] = right
    if n % 2 == 0:
        k = block.shape[split_axis] // 2
        top = lax.ppermute(lax.slice_in_dim(left, 0, k, axis=split_axis), axis, fwd)
        bottom = lax.ppermute(lax.slice_in_dim(right, k, None, axis=split_axis), axis, bwd)
        out[n // 2] = (top, bottom)
    return out


def stacked_ring(block, axis, n, split_axis):
    parts = ring(block, axis, n, split_axis)
    whole = [jnp.concatenate(p, axis=split_axis) if isinstance(p, tuple) else p for p in parts]
    return jnp.stack(whole, axis=0)


def stacked_direct(block, axis, n):
    parts = [block] + [
        lax.ppermute(block, axis, [(j, (j - d) % n) for j in range(n)]) for d in range(1, n)
    ]
    return jnp.stack(parts, axis=0)


def ring_pieces(block, axis, n, split_axis, fold=None, acc=None):
    fwd = [(i, (i + 1) % n) for i in range(n)]
    bwd = [(i, (i - 1) % n) for i in range(n)]
    full = block.shape[split_axis]
    pieces = []

    def take(new):
        nonlocal acc
        pieces.extend(new)
        if fold is not None:
            acc = fold(acc, new)

    take([(0, 0, full, block)])
    left, right = block, block
    for d in range(1, (n + 1) // 2):
        if d > 1 and fold is not None:
            left, right, acc = lax.optimization_barrier((left, right, acc))
        left = lax.ppermute(left, axis, fwd)
        right = lax.ppermute(right, axis, bwd)
        take([(n - d, 0, full, left), (d, 0, full, right)])
    if n % 2 == 0:
        if fold is not None:
            left, right, acc = lax.optimization_barrier((left, right, acc))
        k = full // 2
        top = lax.ppermute(lax.slice_in_dim(left, 0, k, axis=split_axis), axis, fwd)
        bottom = lax.ppermute(lax.slice_in_dim(right, k, None, axis=split_axis), axis, bwd)
        take([(n // 2, 0, k, top), (n // 2, k, full, bottom)])
    return pieces, acc


def reduce_scatter_tp(partial, n_chip):
    rows = partial.shape[0]
    block_cols = partial.shape[1] // (2 * n_chip)
    at_c = lax.axis_index("c")
    at_z = lax.axis_index("zl")
    blocks = partial.reshape(rows, n_chip, 2, block_cols)
    keep = lax.dynamic_index_in_dim(blocks, at_c, axis=2, keepdims=False)
    give = lax.dynamic_index_in_dim(blocks, 1 - at_c, axis=2, keepdims=False)
    got = lax.ppermute(give, "c", [(0, 1), (1, 0)])
    chip_sum = keep.astype(jnp.float32) + got.astype(jnp.float32)
    total = lax.dynamic_index_in_dim(chip_sum, at_z, axis=1, keepdims=False)
    for d in range(1, n_chip):
        for sign in (1, -1):
            route = [(i, i + sign * d) for i in range(n_chip) if 0 <= i + sign * d < n_chip]
            target = jnp.clip(at_z + sign * d, 0, n_chip - 1)
            block = lax.dynamic_index_in_dim(chip_sum, target, axis=1, keepdims=False)
            total = total + lax.ppermute(block.astype(jnp.bfloat16), "zl", route).astype(jnp.float32)
    return total


def norm_scale(value_matrix, gain):
    mean_square = jnp.mean(value_matrix * value_matrix, axis=-1, keepdims=True)
    return value_matrix * lax.rsqrt(mean_square + epsilon) * gain


def rotary(value_matrix, places):
    half_dim = value_matrix.shape[-1] // 2
    inverse = rotary_base ** (-jnp.arange(half_dim, dtype=jnp.float32) / half_dim)
    angles = places.astype(jnp.float32)[:, None] * inverse[None, :]
    cosine = jnp.cos(angles)[:, None, :]
    sine = jnp.sin(angles)[:, None, :]
    first = value_matrix[..., :half_dim]
    second = value_matrix[..., half_dim:]
    return jnp.concatenate(
        [first * cosine - second * sine, second * cosine + first * sine], axis=-1
    )


def local(
    residual,
    input_gain,
    w_query,
    key_weight,
    value_weight,
    query_gain,
    key_gain,
    w_out,
    post_gain,
    positions,
):
    sizes = dict(SEQ_PARTS)
    n_seq = int(np.prod([n for _, n in SEQ_PARTS]))
    tok_rows = residual.shape[0]
    seq_at = lax.axis_index(SEQ)
    tp_at = lax.axis_index(TP)
    head_dim = query_gain.shape[0]
    local_kv = key_weight.shape[1] // head_dim
    query_group = w_query.shape[1] // key_weight.shape[1]
    q_cols = w_query.shape[1]
    k_cols = key_weight.shape[1]
    v_cols = value_weight.shape[1]
    shard_rows = w_query.shape[0]

    nz, ny, nx = sizes["zh"], sizes["y"], sizes["x"]
    gathered = lax.all_gather(residual, TP, axis=1, tiled=True)
    normalized_input = norm_scale(gathered.astype(jnp.float32), input_gain).astype(jnp.bfloat16)
    at_zh, at_y, at_x = (lax.axis_index(name) for name in SEQ)
    rel_y = (at_y + jnp.arange(ny)) % ny
    rel_x = (at_x + jnp.arange(nx)) % nx
    rel_z = (at_zh + jnp.arange(nz)) % nz
    rel_shard = ((rel_z[None, None, :] * ny + rel_y[:, None, None]) * nx + rel_x[None, :, None]).reshape(-1)
    normed_rel = jnp.take(
        normalized_input.reshape(tok_rows, n_seq, shard_rows), rel_shard, axis=1
    ).reshape(tok_rows, ny, nx, nz, shard_rows)

    def contract(lhs, piece):
        return lax.dot_general(
            lhs, piece, (((1, 2, 3), (0, 1, 2)), ((), ())), preferred_element_type=jnp.float32
        )

    def fold_qk(acc, new):
        for dy, lo, hi, piece in new:
            term = contract(normed_rel[:, dy, :, lo:hi], piece)
            acc = term if acc is None else acc + term
        return acc

    def fold_v(acc, new):
        for dx, lo, hi, piece in new:
            term = contract(normed_rel[:, :, dx, lo:hi], piece)
            acc = term if acc is None else acc + term
        return acc

    packed = jnp.concatenate([w_query, key_weight, value_weight, w_out.T], axis=1)
    by_zh = stacked_ring(packed, "zh", nz, 0)
    split = q_cols + k_cols
    half_a = by_zh[:, :, :split]
    half_b = by_zh[:, :, split:]
    a_x = stacked_direct(half_a, "x", nx)
    b_y = stacked_ring(half_b, "y", ny, 0)
    _, qk = ring_pieces(a_x, "y", ny, 1, fold_qk, None)
    b_pieces, b_sum = ring_pieces(b_y, "x", nx, 1, fold_v, None)
    projected_values = b_sum[:, :v_cols]
    queries_raw = qk[:, :q_cols]
    unrotated_keys = qk[:, q_cols:]
    own_places = lax.dynamic_slice_in_dim(positions, seq_at * tok_rows, tok_rows, 0)
    reach = (LOOKBACK_SPAN - 2) // tok_rows + 1

    def attend(query_matrix, stacked, key_places, valid):
        key_matrix = stacked[0].reshape(-1, local_kv, head_dim)
        value_matrix = stacked[1].reshape(-1, local_kv, head_dim)
        scores = (
            jnp.einsum(
                "qkgd,skd->kgqs", query_matrix, key_matrix, preferred_element_type=jnp.float32
            )
            * score_scale
        )
        distance = own_places[:, None] - key_places[None, :]
        allowed = valid[None, :] & (distance >= 0) & (distance < LOOKBACK_SPAN)
        weights = jnp.where(allowed[None, None], jnp.exp(scores), jnp.zeros_like(scores))
        total = jnp.sum(weights, axis=-1)
        summed = jnp.einsum(
            "kgqs,skd->qkgd",
            weights.astype(jnp.bfloat16),
            value_matrix,
            preferred_element_type=jnp.float32,
        )
        return (total, summed)

    key_matrix = rotary(
        norm_scale(unrotated_keys.reshape(tok_rows, local_kv, head_dim), key_gain), own_places
    )
    stacked = jnp.stack(
        [key_matrix.reshape(tok_rows, local_kv * head_dim), projected_values]
    ).astype(jnp.bfloat16)
    pieces = []
    for distance in range(reach, 0, -1):
        pieces.append(from_behind(stacked, SEQ, n_seq, distance))
    halo = jnp.concatenate(pieces, axis=1)
    query_matrix = rotary(
        norm_scale(queries_raw.reshape(tok_rows, local_kv * query_group, head_dim), query_gain),
        own_places,
    )
    query_matrix = query_matrix.astype(jnp.bfloat16).reshape(
        tok_rows, local_kv, query_group, head_dim
    )
    inner_total, inner_sum = attend(
        query_matrix, stacked, own_places, jnp.ones((tok_rows,), jnp.bool_)
    )
    span = halo.shape[1]
    padded_places = jnp.concatenate([jnp.zeros((span,), jnp.int32), positions])
    halo_places = lax.dynamic_slice_in_dim(padded_places, seq_at * tok_rows, span, 0)
    halo_valid = seq_at * tok_rows - span + jnp.arange(span, dtype=jnp.int32) >= 0
    outer_total, outer_sum = attend(query_matrix, halo, halo_places, halo_valid)
    total = jnp.transpose(inner_total + outer_total, (2, 0, 1))
    merged = (inner_sum + outer_sum) / total[..., None]
    attended = merged.astype(jnp.bfloat16).reshape(tok_rows, local_kv * query_group * head_dim)
    out_rel = jnp.zeros((tok_rows, ny, nx, nz, shard_rows), jnp.bfloat16)
    attended_wide = jnp.concatenate(
        [jnp.zeros((tok_rows, v_cols), attended.dtype), attended], axis=1
    )
    for dx, lo, hi, piece in b_pieces:
        cols = lax.dot_general(
            attended_wide,
            piece,
            (((1,), (3,)), ((), ())),
            preferred_element_type=jnp.float32,
        )
        out_rel = out_rel.at[:, :, dx, lo:hi].set(cols.astype(jnp.bfloat16))
    abs_z, abs_y, abs_x = jnp.unravel_index(jnp.arange(n_seq), (nz, ny, nx))
    abs_rel = (((abs_y - at_y) % ny) * nx + (abs_x - at_x) % nx) * nz + (abs_z - at_zh) % nz
    partial_out = jnp.take(
        out_rel.reshape(tok_rows, n_seq, shard_rows), abs_rel, axis=1
    ).reshape(tok_rows, n_seq * shard_rows)
    summed_cols = reduce_scatter_tp(partial_out, dict(TP_PARTS)["zl"])
    full_width = post_gain.shape[0]
    squares = lax.psum(jnp.sum(summed_cols * summed_cols, axis=1), TP)
    inverse_rms = lax.rsqrt(squares / full_width + epsilon)
    gain_part = lax.dynamic_slice_in_dim(
        post_gain, tp_at * summed_cols.shape[1], summed_cols.shape[1], 0
    )
    return (residual.astype(jnp.float32) + summed_cols * inverse_rms[:, None] * gain_part).astype(
        jnp.bfloat16
    )


def solution(mesh):
    seq_n, tp_n = mesh.devices.shape
    shape = tuple(n for _, n in SEQ_PARTS) + tuple(n for _, n in TP_PARTS)
    assert int(np.prod(shape[:3])) == seq_n and int(np.prod(shape[3:])) == tp_n
    fine = Mesh(mesh.devices.reshape(shape), SEQ + TP)
    blocked = P(SEQ, TP)
    in_specs = (
        blocked,
        P(),
        blocked,
        blocked,
        blocked,
        P(),
        P(),
        P(TP, SEQ),
        P(),
        P(),
    )
    return jax.shard_map(local, mesh=fine, in_specs=in_specs, out_specs=blocked, check_vma=False)
```

```python
import jax
import jax.numpy as jnp
import numpy as np
from jax import lax
from jax.sharding import Mesh
from jax.sharding import PartitionSpec as P

LOOKBACK_SPAN = 1024

SEQ_PARTS = (("zh", 2), ("y", 8), ("x", 4))
TP_PARTS = (("zl", 4), ("c", 2))
SEQ = tuple(name for name, _ in SEQ_PARTS)
TP = tuple(name for name, _ in TP_PARTS)

epsilon = 1e-06
score_scale = 168.0 ** (-0.5)
rotary_base = 10000.0


def from_behind(block, axis, n, distance):
    route = [(i - distance, i) for i in range(n) if i - distance >= 0]
    return lax.ppermute(block, axis, route)


def ring(block, axis, n, split_axis):
    if n == 1:
        return [block]
    fwd = [(i, (i + 1) % n) for i in range(n)]
    bwd = [(i, (i - 1) % n) for i in range(n)]
    if n == 2:
        return [block, lax.ppermute(block, axis, fwd)]
    out = [None] * n
    out[0] = block
    left, right = block, block
    for d in range(1, (n + 1) // 2):
        left = lax.ppermute(left, axis, fwd)
        right = lax.ppermute(right, axis, bwd)
        out[n - d] = left
        out[d] = right
    if n % 2 == 0:
        k = block.shape[split_axis] // 2
        top = lax.ppermute(lax.slice_in_dim(left, 0, k, axis=split_axis), axis, fwd)
        bottom = lax.ppermute(lax.slice_in_dim(right, k, None, axis=split_axis), axis, bwd)
        out[n // 2] = (top, bottom)
    return out


def stacked_ring(block, axis, n, split_axis):
    parts = ring(block, axis, n, split_axis)
    whole = [jnp.concatenate(p, axis=split_axis) if isinstance(p, tuple) else p for p in parts]
    return jnp.stack(whole, axis=0)


def stacked_direct(block, axis, n):
    parts = [block] + [
        lax.ppermute(block, axis, [(j, (j - d) % n) for j in range(n)]) for d in range(1, n)
    ]
    return jnp.stack(parts, axis=0)


def ring_pieces(block, axis, n, split_axis, fold=None, acc=None):
    fwd = [(i, (i + 1) % n) for i in range(n)]
    bwd = [(i, (i - 1) % n) for i in range(n)]
    full = block.shape[split_axis]
    pieces = []

    def take(new):
        nonlocal acc
        pieces.extend(new)
        if fold is not None:
            acc = fold(acc, new)

    take([(0, 0, full, block)])
    left, right = block, block
    for d in range(1, (n + 1) // 2):
        if d > 1 and fold is not None:
            left, right, acc = lax.optimization_barrier((left, right, acc))
        left = lax.ppermute(left, axis, fwd)
        right = lax.ppermute(right, axis, bwd)
        take([(n - d, 0, full, left), (d, 0, full, right)])
    if n % 2 == 0:
        if fold is not None:
            left, right, acc = lax.optimization_barrier((left, right, acc))
        k = full // 2
        top = lax.ppermute(lax.slice_in_dim(left, 0, k, axis=split_axis), axis, fwd)
        bottom = lax.ppermute(lax.slice_in_dim(right, k, None, axis=split_axis), axis, bwd)
        take([(n // 2, 0, k, top), (n // 2, k, full, bottom)])
    return pieces, acc


def reduce_scatter_tp(partial, n_chip):
    rows = partial.shape[0]
    block_cols = partial.shape[1] // (2 * n_chip)
    at_c = lax.axis_index("c")
    at_z = lax.axis_index("zl")
    blocks = partial.reshape(rows, n_chip, 2, block_cols)
    keep = lax.dynamic_index_in_dim(blocks, at_c, axis=2, keepdims=False)
    give = lax.dynamic_index_in_dim(blocks, 1 - at_c, axis=2, keepdims=False)
    got = lax.ppermute(give, "c", [(0, 1), (1, 0)])
    chip_sum = keep.astype(jnp.float32) + got.astype(jnp.float32)
    total = lax.dynamic_index_in_dim(chip_sum, at_z, axis=1, keepdims=False)
    for d in range(1, n_chip):
        for sign in (1, -1):
            route = [(i, i + sign * d) for i in range(n_chip) if 0 <= i + sign * d < n_chip]
            target = jnp.clip(at_z + sign * d, 0, n_chip - 1)
            block = lax.dynamic_index_in_dim(chip_sum, target, axis=1, keepdims=False)
            total = total + lax.ppermute(block.astype(jnp.bfloat16), "zl", route).astype(jnp.float32)
    return total


def norm_scale(value_matrix, gain):
    mean_square = jnp.mean(value_matrix * value_matrix, axis=-1, keepdims=True)
    return value_matrix * lax.rsqrt(mean_square + epsilon) * gain


def rotary(value_matrix, places):
    half_dim = value_matrix.shape[-1] // 2
    inverse = rotary_base ** (-jnp.arange(half_dim, dtype=jnp.float32) / half_dim)
    angles = places.astype(jnp.float32)[:, None] * inverse[None, :]
    cosine = jnp.cos(angles)[:, None, :]
    sine = jnp.sin(angles)[:, None, :]
    first = value_matrix[..., :half_dim]
    second = value_matrix[..., half_dim:]
    return jnp.concatenate(
        [first * cosine - second * sine, second * cosine + first * sine], axis=-1
    )


def local(
    residual,
    input_gain,
    w_query,
    key_weight,
    value_weight,
    query_gain,
    key_gain,
    w_out,
    post_gain,
    positions,
):
    sizes = dict(SEQ_PARTS)
    n_seq = int(np.prod([n for _, n in SEQ_PARTS]))
    tok_rows = residual.shape[0]
    seq_at = lax.axis_index(SEQ)
    tp_at = lax.axis_index(TP)
    head_dim = query_gain.shape[0]
    local_kv = key_weight.shape[1] // head_dim
    query_group = w_query.shape[1] // key_weight.shape[1]
    q_cols = w_query.shape[1]
    k_cols = key_weight.shape[1]
    v_cols = value_weight.shape[1]
    shard_rows = w_query.shape[0]

    nz, ny, nx = sizes["zh"], sizes["y"], sizes["x"]
    gathered = lax.all_gather(residual, TP, axis=1, tiled=True)
    normalized_input = norm_scale(gathered.astype(jnp.float32), input_gain).astype(jnp.bfloat16)
    at_zh, at_y, at_x = (lax.axis_index(name) for name in SEQ)
    normed_rel = normalized_input.reshape(tok_rows, nz, ny, nx, shard_rows).transpose(0, 2, 3, 1, 4)
    normed_rel = jnp.roll(normed_rel, -at_y, axis=1)
    normed_rel = jnp.roll(normed_rel, -at_x, axis=2)
    normed_rel = jnp.roll(normed_rel, -at_zh, axis=3)

    def contract(lhs, piece):
        return lax.dot_general(
            lhs, piece, (((1, 2, 3), (0, 1, 2)), ((), ())), preferred_element_type=jnp.float32
        )

    def fold_qk(acc, new):
        for dy, lo, hi, piece in new:
            term = contract(normed_rel[:, dy, lo:hi], piece)
            acc = term if acc is None else acc + term
        return acc

    def fold_v(acc, new):
        for dx, lo, hi, piece in new:
            term = contract(normed_rel[:, lo:hi, dx], piece[..., :v_cols])
            acc = term if acc is None else acc + term
        return acc

    packed = jnp.concatenate([w_query, key_weight, value_weight, w_out.T], axis=1)
    by_zh = stacked_ring(packed, "zh", nz, 0)
    split = q_cols + k_cols
    half_a = by_zh[:, :, :split]
    half_b = by_zh[:, :, split:]
    a_x = stacked_direct(half_a, "x", nx)
    b_y = stacked_ring(half_b, "y", ny, 0)
    _, qk = ring_pieces(a_x, "y", ny, 0, fold_qk, None)
    b_pieces, projected_values = ring_pieces(b_y, "x", nx, 0, fold_v, None)
    queries_raw = qk[:, :q_cols]
    unrotated_keys = qk[:, q_cols:]
    own_places = lax.dynamic_slice_in_dim(positions, seq_at * tok_rows, tok_rows, 0)
    reach = (LOOKBACK_SPAN - 2) // tok_rows + 1

    def attend(query_matrix, stacked, key_places, valid):
        key_matrix = stacked[0].reshape(-1, local_kv, head_dim)
        value_matrix = stacked[1].reshape(-1, local_kv, head_dim)
        scores = (
            jnp.einsum(
                "qkgd,skd->kgqs", query_matrix, key_matrix, preferred_element_type=jnp.float32
            )
            * score_scale
        )
        distance = own_places[:, None] - key_places[None, :]
        allowed = valid[None, :] & (distance >= 0) & (distance < LOOKBACK_SPAN)
        weights = jnp.where(allowed[None, None], jnp.exp(scores), jnp.zeros_like(scores))
        total = jnp.sum(weights, axis=-1)
        summed = jnp.einsum(
            "kgqs,skd->qkgd",
            weights.astype(jnp.bfloat16),
            value_matrix,
            preferred_element_type=jnp.float32,
        )
        return (total, summed)

    key_matrix = rotary(
        norm_scale(unrotated_keys.reshape(tok_rows, local_kv, head_dim), key_gain), own_places
    )
    stacked = jnp.stack(
        [key_matrix.reshape(tok_rows, local_kv * head_dim), projected_values]
    ).astype(jnp.bfloat16)
    pieces = []
    for distance in range(reach, 0, -1):
        pieces.append(from_behind(stacked, SEQ, n_seq, distance))
    halo = jnp.concatenate(pieces, axis=1)
    query_matrix = rotary(
        norm_scale(queries_raw.reshape(tok_rows, local_kv * query_group, head_dim), query_gain),
        own_places,
    )
    query_matrix = query_matrix.astype(jnp.bfloat16).reshape(
        tok_rows, local_kv, query_group, head_dim
    )
    inner_total, inner_sum = attend(
        query_matrix, stacked, own_places, jnp.ones((tok_rows,), jnp.bool_)
    )
    span = halo.shape[1]
    padded_places = jnp.concatenate([jnp.zeros((span,), jnp.int32), positions])
    halo_places = lax.dynamic_slice_in_dim(padded_places, seq_at * tok_rows, span, 0)
    halo_valid = seq_at * tok_rows - span + jnp.arange(span, dtype=jnp.int32) >= 0
    outer_total, outer_sum = attend(query_matrix, halo, halo_places, halo_valid)
    total = jnp.transpose(inner_total + outer_total, (2, 0, 1))
    merged = (inner_sum + outer_sum) / total[..., None]
    attended = merged.astype(jnp.bfloat16).reshape(tok_rows, local_kv * query_group * head_dim)
    out_rel = jnp.zeros((tok_rows, ny, nx, nz, shard_rows), jnp.bfloat16)
    for dx, lo, hi, piece in b_pieces:
        cols = lax.dot_general(
            attended,
            piece[..., v_cols:],
            (((1,), (3,)), ((), ())),
            preferred_element_type=jnp.float32,
        )
        out_rel = out_rel.at[:, lo:hi, dx].set(cols.astype(jnp.bfloat16))
    out_abs = jnp.roll(out_rel, at_y, axis=1)
    out_abs = jnp.roll(out_abs, at_x, axis=2)
    out_abs = jnp.roll(out_abs, at_zh, axis=3)
    partial_out = out_abs.transpose(0, 3, 1, 2, 4).reshape(tok_rows, n_seq * shard_rows)
    summed_cols = reduce_scatter_tp(partial_out, dict(TP_PARTS)["zl"])
    full_width = post_gain.shape[0]
    own_squares = jnp.sum(summed_cols * summed_cols, axis=1)
    pair_squares = own_squares + lax.ppermute(own_squares, "c", [(0, 1), (1, 0)])
    squares = lax.psum(pair_squares, "zl")
    inverse_rms = lax.rsqrt(squares / full_width + epsilon)
    gain_part = lax.dynamic_slice_in_dim(
        post_gain, tp_at * summed_cols.shape[1], summed_cols.shape[1], 0
    )
    return (residual.astype(jnp.float32) + summed_cols * inverse_rms[:, None] * gain_part).astype(
        jnp.bfloat16
    )


def solution(mesh):
    seq_n, tp_n = mesh.devices.shape
    shape = tuple(n for _, n in SEQ_PARTS) + tuple(n for _, n in TP_PARTS)
    assert int(np.prod(shape[:3])) == seq_n and int(np.prod(shape[3:])) == tp_n
    fine = Mesh(mesh.devices.reshape(shape), SEQ + TP)
    blocked = P(SEQ, TP)
    in_specs = (
        blocked,
        P(),
        blocked,
        blocked,
        blocked,
        P(),
        P(),
        P(TP, SEQ),
        P(),
        P(),
    )
    return jax.shard_map(local, mesh=fine, in_specs=in_specs, out_specs=blocked, check_vma=False)
```

```python
import jax
import jax.numpy as jnp
import numpy as np
from jax import lax
from jax.sharding import Mesh
from jax.sharding import PartitionSpec as P

LOOKBACK_SPAN = 1024

SEQ_PARTS = (("zh", 2), ("y", 8), ("x", 4))
TP_PARTS = (("zl", 4), ("c", 2))
SEQ = tuple(name for name, _ in SEQ_PARTS)
TP = tuple(name for name, _ in TP_PARTS)

epsilon = 1e-06
score_scale = 168.0 ** (-0.5)
rotary_base = 10000.0


def from_behind(block, axis, n, distance):
    route = [(i - distance, i) for i in range(n) if i - distance >= 0]
    return lax.ppermute(block, axis, route)


def ring(block, axis, n, split_axis):
    if n == 1:
        return [block]
    fwd = [(i, (i + 1) % n) for i in range(n)]
    bwd = [(i, (i - 1) % n) for i in range(n)]
    if n == 2:
        return [block, lax.ppermute(block, axis, fwd)]
    out = [None] * n
    out[0] = block
    left, right = block, block
    for d in range(1, (n + 1) // 2):
        left = lax.ppermute(left, axis, fwd)
        right = lax.ppermute(right, axis, bwd)
        out[n - d] = left
        out[d] = right
    if n % 2 == 0:
        k = block.shape[split_axis] // 2
        top = lax.ppermute(lax.slice_in_dim(left, 0, k, axis=split_axis), axis, fwd)
        bottom = lax.ppermute(lax.slice_in_dim(right, k, None, axis=split_axis), axis, bwd)
        out[n // 2] = (top, bottom)
    return out


def stacked_ring(block, axis, n, split_axis):
    parts = ring(block, axis, n, split_axis)
    whole = [jnp.concatenate(p, axis=split_axis) if isinstance(p, tuple) else p for p in parts]
    return jnp.stack(whole, axis=0)


def stacked_direct(block, axis, n):
    parts = [block] + [
        lax.ppermute(block, axis, [(j, (j - d) % n) for j in range(n)]) for d in range(1, n)
    ]
    return jnp.stack(parts, axis=0)


def ring_pieces(block, axis, n, split_axis, fold=None, acc=None):
    fwd = [(i, (i + 1) % n) for i in range(n)]
    bwd = [(i, (i - 1) % n) for i in range(n)]
    full = block.shape[split_axis]
    pieces = []

    def take(new):
        nonlocal acc
        pieces.extend(new)
        if fold is not None:
            acc = fold(acc, new)

    take([(0, 0, full, block)])
    left, right = block, block
    for d in range(1, (n + 1) // 2):
        if d > 1 and fold is not None:
            left, right, acc = lax.optimization_barrier((left, right, acc))
        left = lax.ppermute(left, axis, fwd)
        right = lax.ppermute(right, axis, bwd)
        take([(n - d, 0, full, left), (d, 0, full, right)])
    if n % 2 == 0:
        if fold is not None:
            left, right, acc = lax.optimization_barrier((left, right, acc))
        k = full // 2
        top = lax.ppermute(lax.slice_in_dim(left, 0, k, axis=split_axis), axis, fwd)
        bottom = lax.ppermute(lax.slice_in_dim(right, k, None, axis=split_axis), axis, bwd)
        take([(n // 2, 0, k, top), (n // 2, k, full, bottom)])
    return pieces, acc


def reduce_scatter_tp(partial, n_chip):
    rows = partial.shape[0]
    block_cols = partial.shape[1] // (2 * n_chip)
    at_c = lax.axis_index("c")
    at_z = lax.axis_index("zl")
    blocks = partial.reshape(rows, n_chip, 2, block_cols)
    keep = lax.dynamic_index_in_dim(blocks, at_c, axis=2, keepdims=False)
    give = lax.dynamic_index_in_dim(blocks, 1 - at_c, axis=2, keepdims=False)
    got = lax.ppermute(give, "c", [(0, 1), (1, 0)])
    chip_sum = keep.astype(jnp.float32) + got.astype(jnp.float32)
    total = lax.dynamic_index_in_dim(chip_sum, at_z, axis=1, keepdims=False)
    for d in range(1, n_chip):
        for sign in (1, -1):
            route = [(i, i + sign * d) for i in range(n_chip) if 0 <= i + sign * d < n_chip]
            target = jnp.clip(at_z + sign * d, 0, n_chip - 1)
            block = lax.dynamic_index_in_dim(chip_sum, target, axis=1, keepdims=False)
            total = total + lax.ppermute(block.astype(jnp.bfloat16), "zl", route).astype(jnp.float32)
    return total


def all_gather_tp(block, n_chip):
    at_c = lax.axis_index("c")
    at_z = lax.axis_index("zl")
    other = lax.ppermute(block, "c", [(0, 1), (1, 0)])
    chip_block = jnp.where(
        at_c == 0, jnp.concatenate([block, other], axis=1), jnp.concatenate([other, block], axis=1)
    )
    below = [
        lax.ppermute(chip_block, "zl", [(i, i + d) for i in range(n_chip - d)])
        for d in range(1, n_chip)
    ]
    above = [
        lax.ppermute(chip_block, "zl", [(i, i - d) for i in range(d, n_chip)])
        for d in range(1, n_chip)
    ]
    candidates = jnp.stack([chip_block] + below + above, axis=0)
    offset = jnp.arange(n_chip) - at_z
    pick = jnp.where(offset == 0, 0, jnp.where(offset < 0, -offset, n_chip - 1 + offset))
    chips = jnp.take(candidates, pick, axis=0)
    return chips.transpose(1, 0, 2).reshape(block.shape[0], n_chip * chip_block.shape[1])


def norm_scale(value_matrix, gain):
    mean_square = jnp.mean(value_matrix * value_matrix, axis=-1, keepdims=True)
    return value_matrix * lax.rsqrt(mean_square + epsilon) * gain


def rotary(value_matrix, places):
    half_dim = value_matrix.shape[-1] // 2
    inverse = rotary_base ** (-jnp.arange(half_dim, dtype=jnp.float32) / half_dim)
    angles = places.astype(jnp.float32)[:, None] * inverse[None, :]
    cosine = jnp.cos(angles)[:, None, :]
    sine = jnp.sin(angles)[:, None, :]
    first = value_matrix[..., :half_dim]
    second = value_matrix[..., half_dim:]
    return jnp.concatenate(
        [first * cosine - second * sine, second * cosine + first * sine], axis=-1
    )


def local(
    residual,
    input_gain,
    w_query,
    key_weight,
    value_weight,
    query_gain,
    key_gain,
    w_out,
    post_gain,
    positions,
):
    sizes = dict(SEQ_PARTS)
    n_seq = int(np.prod([n for _, n in SEQ_PARTS]))
    tok_rows = residual.shape[0]
    seq_at = lax.axis_index(SEQ)
    tp_at = lax.axis_index(TP)
    head_dim = query_gain.shape[0]
    local_kv = key_weight.shape[1] // head_dim
    query_group = w_query.shape[1] // key_weight.shape[1]
    q_cols = w_query.shape[1]
    k_cols = key_weight.shape[1]
    v_cols = value_weight.shape[1]
    shard_rows = w_query.shape[0]

    nz, ny, nx = sizes["zh"], sizes["y"], sizes["x"]
    gathered = all_gather_tp(residual, dict(TP_PARTS)["zl"])
    normalized_input = norm_scale(gathered.astype(jnp.float32), input_gain).astype(jnp.bfloat16)
    at_zh, at_y, at_x = (lax.axis_index(name) for name in SEQ)
    normed_rel = normalized_input.reshape(tok_rows, nz, ny, nx, shard_rows).transpose(0, 2, 3, 1, 4)
    normed_rel = jnp.roll(normed_rel, -at_y, axis=1)
    normed_rel = jnp.roll(normed_rel, -at_x, axis=2)
    normed_rel = jnp.roll(normed_rel, -at_zh, axis=3)

    def contract(lhs, piece):
        return lax.dot_general(
            lhs, piece, (((1, 2, 3), (0, 1, 2)), ((), ())), preferred_element_type=jnp.float32
        )

    def fold_qk(acc, new):
        for dy, lo, hi, piece in new:
            term = contract(normed_rel[:, dy, lo:hi], piece)
            acc = term if acc is None else acc + term
        return acc

    def fold_v(acc, new):
        for dx, lo, hi, piece in new:
            term = contract(normed_rel[:, lo:hi, dx], piece[..., :v_cols])
            acc = term if acc is None else acc + term
        return acc

    packed = jnp.concatenate([w_query, key_weight, value_weight, w_out.T], axis=1)
    by_zh = stacked_ring(packed, "zh", nz, 0)
    split = q_cols + k_cols
    half_a = by_zh[:, :, :split]
    half_b = by_zh[:, :, split:]
    a_x = stacked_direct(half_a, "x", nx)
    b_y = stacked_ring(half_b, "y", ny, 0)
    _, qk = ring_pieces(a_x, "y", ny, 0, fold_qk, None)
    b_pieces, projected_values = ring_pieces(b_y, "x", nx, 0, fold_v, None)
    queries_raw = qk[:, :q_cols]
    unrotated_keys = qk[:, q_cols:]
    own_places = lax.dynamic_slice_in_dim(positions, seq_at * tok_rows, tok_rows, 0)
    reach = (LOOKBACK_SPAN - 2) // tok_rows + 1

    def attend(query_matrix, stacked, key_places, valid):
        key_matrix = stacked[0].reshape(-1, local_kv, head_dim)
        value_matrix = stacked[1].reshape(-1, local_kv, head_dim)
        scores = (
            jnp.einsum(
                "qkgd,skd->kgqs", query_matrix, key_matrix, preferred_element_type=jnp.float32
            )
            * score_scale
        )
        distance = own_places[:, None] - key_places[None, :]
        allowed = valid[None, :] & (distance >= 0) & (distance < LOOKBACK_SPAN)
        weights = jnp.where(allowed[None, None], jnp.exp(scores), jnp.zeros_like(scores))
        total = jnp.sum(weights, axis=-1)
        summed = jnp.einsum(
            "kgqs,skd->qkgd",
            weights.astype(jnp.bfloat16),
            value_matrix,
            preferred_element_type=jnp.float32,
        )
        return (total, summed)

    key_matrix = rotary(
        norm_scale(unrotated_keys.reshape(tok_rows, local_kv, head_dim), key_gain), own_places
    )
    stacked = jnp.stack(
        [key_matrix.reshape(tok_rows, local_kv * head_dim), projected_values]
    ).astype(jnp.bfloat16)
    pieces = []
    for distance in range(reach, 0, -1):
        pieces.append(from_behind(stacked, SEQ, n_seq, distance))
    halo = jnp.concatenate(pieces, axis=1)
    query_matrix = rotary(
        norm_scale(queries_raw.reshape(tok_rows, local_kv * query_group, head_dim), query_gain),
        own_places,
    )
    query_matrix = query_matrix.astype(jnp.bfloat16).reshape(
        tok_rows, local_kv, query_group, head_dim
    )
    inner_total, inner_sum = attend(
        query_matrix, stacked, own_places, jnp.ones((tok_rows,), jnp.bool_)
    )
    span = halo.shape[1]
    padded_places = jnp.concatenate([jnp.zeros((span,), jnp.int32), positions])
    halo_places = lax.dynamic_slice_in_dim(padded_places, seq_at * tok_rows, span, 0)
    halo_valid = seq_at * tok_rows - span + jnp.arange(span, dtype=jnp.int32) >= 0
    outer_total, outer_sum = attend(query_matrix, halo, halo_places, halo_valid)
    total = jnp.transpose(inner_total + outer_total, (2, 0, 1))
    merged = (inner_sum + outer_sum) / total[..., None]
    attended = merged.astype(jnp.bfloat16).reshape(tok_rows, local_kv * query_group * head_dim)
    out_rel = jnp.zeros((tok_rows, ny, nx, nz, shard_rows), jnp.bfloat16)
    for dx, lo, hi, piece in b_pieces:
        cols = lax.dot_general(
            attended,
            piece[..., v_cols:],
            (((1,), (3,)), ((), ())),
            preferred_element_type=jnp.float32,
        )
        out_rel = out_rel.at[:, lo:hi, dx].set(cols.astype(jnp.bfloat16))
    out_abs = jnp.roll(out_rel, at_y, axis=1)
    out_abs = jnp.roll(out_abs, at_x, axis=2)
    out_abs = jnp.roll(out_abs, at_zh, axis=3)
    partial_out = out_abs.transpose(0, 3, 1, 2, 4).reshape(tok_rows, n_seq * shard_rows)
    summed_cols = reduce_scatter_tp(partial_out, dict(TP_PARTS)["zl"])
    full_width = post_gain.shape[0]
    own_squares = jnp.sum(summed_cols * summed_cols, axis=1)
    pair_squares = own_squares + lax.ppermute(own_squares, "c", [(0, 1), (1, 0)])
    squares = lax.psum(pair_squares, "zl")
    inverse_rms = lax.rsqrt(squares / full_width + epsilon)
    gain_part = lax.dynamic_slice_in_dim(
        post_gain, tp_at * summed_cols.shape[1], summed_cols.shape[1], 0
    )
    return (residual.astype(jnp.float32) + summed_cols * inverse_rms[:, None] * gain_part).astype(
        jnp.bfloat16
    )


def solution(mesh):
    seq_n, tp_n = mesh.devices.shape
    shape = tuple(n for _, n in SEQ_PARTS) + tuple(n for _, n in TP_PARTS)
    assert int(np.prod(shape[:3])) == seq_n and int(np.prod(shape[3:])) == tp_n
    fine = Mesh(mesh.devices.reshape(shape), SEQ + TP)
    blocked = P(SEQ, TP)
    in_specs = (
        blocked,
        P(),
        blocked,
        blocked,
        blocked,
        P(),
        P(),
        P(TP, SEQ),
        P(),
        P(),
    )
    return jax.shard_map(local, mesh=fine, in_specs=in_specs, out_specs=blocked, check_vma=False)
```

```python
import jax
import jax.numpy as jnp
import numpy as np
from jax import lax
from jax.sharding import Mesh
from jax.sharding import PartitionSpec as P

LOOKBACK_SPAN = 1024

SEQ_PARTS = (("zh", 2), ("y", 8), ("x", 4))
TP_PARTS = (("zl", 4), ("c", 2))
SEQ = tuple(name for name, _ in SEQ_PARTS)
TP = tuple(name for name, _ in TP_PARTS)

epsilon = 1e-06
score_scale = 168.0 ** (-0.5)
rotary_base = 10000.0


def from_behind(block, axis, n, distance):
    route = [(i - distance, i) for i in range(n) if i - distance >= 0]
    return lax.ppermute(block, axis, route)


def ring(block, axis, n, split_axis):
    if n == 1:
        return [block]
    fwd = [(i, (i + 1) % n) for i in range(n)]
    bwd = [(i, (i - 1) % n) for i in range(n)]
    if n == 2:
        return [block, lax.ppermute(block, axis, fwd)]
    out = [None] * n
    out[0] = block
    left, right = block, block
    for d in range(1, (n + 1) // 2):
        left = lax.ppermute(left, axis, fwd)
        right = lax.ppermute(right, axis, bwd)
        out[n - d] = left
        out[d] = right
    if n % 2 == 0:
        k = block.shape[split_axis] // 2
        top = lax.ppermute(lax.slice_in_dim(left, 0, k, axis=split_axis), axis, fwd)
        bottom = lax.ppermute(lax.slice_in_dim(right, k, None, axis=split_axis), axis, bwd)
        out[n // 2] = (top, bottom)
    return out


def stacked_ring(block, axis, n, split_axis):
    parts = ring(block, axis, n, split_axis)
    whole = [jnp.concatenate(p, axis=split_axis) if isinstance(p, tuple) else p for p in parts]
    return jnp.stack(whole, axis=0)


def stacked_direct(block, axis, n):
    parts = [block] + [
        lax.ppermute(block, axis, [(j, (j - d) % n) for j in range(n)]) for d in range(1, n)
    ]
    return jnp.stack(parts, axis=0)


def ring_pieces(block, axis, n, split_axis, fold=None, acc=None):
    fwd = [(i, (i + 1) % n) for i in range(n)]
    bwd = [(i, (i - 1) % n) for i in range(n)]
    full = block.shape[split_axis]
    pieces = []

    def take(new):
        nonlocal acc
        pieces.extend(new)
        if fold is not None:
            acc = fold(acc, new)

    take([(0, 0, full, block)])
    left, right = block, block
    for d in range(1, (n + 1) // 2):
        if d > 1 and fold is not None:
            left, right, acc = lax.optimization_barrier((left, right, acc))
        left = lax.ppermute(left, axis, fwd)
        right = lax.ppermute(right, axis, bwd)
        take([(n - d, 0, full, left), (d, 0, full, right)])
    if n % 2 == 0:
        if fold is not None:
            left, right, acc = lax.optimization_barrier((left, right, acc))
        k = full // 2
        top = lax.ppermute(lax.slice_in_dim(left, 0, k, axis=split_axis), axis, fwd)
        bottom = lax.ppermute(lax.slice_in_dim(right, k, None, axis=split_axis), axis, bwd)
        take([(n // 2, 0, k, top), (n // 2, k, full, bottom)])
    return pieces, acc


def reduce_scatter_tp(partial, n_chip):
    rows = partial.shape[0]
    block_cols = partial.shape[1] // (2 * n_chip)
    at_c = lax.axis_index("c")
    at_z = lax.axis_index("zl")
    blocks = partial.reshape(rows, n_chip, 2, block_cols)
    keep = lax.dynamic_index_in_dim(blocks, at_c, axis=2, keepdims=False)
    give = lax.dynamic_index_in_dim(blocks, 1 - at_c, axis=2, keepdims=False)
    got = lax.ppermute(give, "c", [(0, 1), (1, 0)])
    chip_sum = keep.astype(jnp.float32) + got.astype(jnp.float32)
    total = lax.dynamic_index_in_dim(chip_sum, at_z, axis=1, keepdims=False)
    for d in range(1, n_chip):
        for sign in (1, -1):
            route = [(i, i + sign * d) for i in range(n_chip) if 0 <= i + sign * d < n_chip]
            target = jnp.clip(at_z + sign * d, 0, n_chip - 1)
            block = lax.dynamic_index_in_dim(chip_sum, target, axis=1, keepdims=False)
            total = total + lax.ppermute(block.astype(jnp.bfloat16), "zl", route).astype(jnp.float32)
    return total


def norm_scale(value_matrix, gain):
    mean_square = jnp.mean(value_matrix * value_matrix, axis=-1, keepdims=True)
    return value_matrix * lax.rsqrt(mean_square + epsilon) * gain


def rotary(value_matrix, places):
    half_dim = value_matrix.shape[-1] // 2
    inverse = rotary_base ** (-jnp.arange(half_dim, dtype=jnp.float32) / half_dim)
    angles = places.astype(jnp.float32)[:, None] * inverse[None, :]
    cosine = jnp.cos(angles)[:, None, :]
    sine = jnp.sin(angles)[:, None, :]
    first = value_matrix[..., :half_dim]
    second = value_matrix[..., half_dim:]
    return jnp.concatenate(
        [first * cosine - second * sine, second * cosine + first * sine], axis=-1
    )


def local(
    residual,
    input_gain,
    w_query,
    key_weight,
    value_weight,
    query_gain,
    key_gain,
    w_out,
    post_gain,
    positions,
):
    sizes = dict(SEQ_PARTS)
    n_seq = int(np.prod([n for _, n in SEQ_PARTS]))
    tok_rows = residual.shape[0]
    seq_at = lax.axis_index(SEQ)
    tp_at = lax.axis_index(TP)
    head_dim = query_gain.shape[0]
    local_kv = key_weight.shape[1] // head_dim
    query_group = w_query.shape[1] // key_weight.shape[1]
    q_cols = w_query.shape[1]
    k_cols = key_weight.shape[1]
    v_cols = value_weight.shape[1]
    shard_rows = w_query.shape[0]

    nz, ny, nx = sizes["zh"], sizes["y"], sizes["x"]
    gathered = lax.all_gather(residual, TP, axis=1, tiled=True)
    normalized_input = norm_scale(gathered.astype(jnp.float32), input_gain).astype(jnp.bfloat16)
    at_zh, at_y, at_x = (lax.axis_index(name) for name in SEQ)
    normed_rel = normalized_input.reshape(tok_rows, nz, ny, nx, shard_rows).transpose(0, 2, 3, 1, 4)
    normed_rel = jnp.roll(normed_rel, -at_y, axis=1)
    normed_rel = jnp.roll(normed_rel, -at_x, axis=2)
    normed_rel = jnp.roll(normed_rel, -at_zh, axis=3)

    def contract(lhs, piece):
        return lax.dot_general(
            lhs, piece, (((1, 2, 3), (0, 1, 2)), ((), ())), preferred_element_type=jnp.float32
        )

    def fold_qk(acc, new):
        for dy, lo, hi, piece in new:
            term = contract(normed_rel[:, dy, lo:hi], piece)
            acc = term if acc is None else acc + term
        return acc

    def fold_v(acc, new):
        for dx, lo, hi, piece in new:
            term = contract(normed_rel[:, lo:hi, dx], piece[..., :v_cols])
            acc = term if acc is None else acc + term
        return acc

    packed = jnp.concatenate([w_query, key_weight, value_weight, w_out.T], axis=1)
    by_zh = stacked_ring(packed, "zh", nz, 0)
    split = q_cols + k_cols
    half_a = by_zh[:, :, :split]
    half_b = by_zh[:, :, split:]
    a_x = stacked_direct(half_a, "x", nx)
    b_y = stacked_ring(half_b, "y", ny, 0)
    _, qk = ring_pieces(a_x, "y", ny, 0, fold_qk, None)
    b_pieces, projected_values = ring_pieces(b_y, "x", nx, 0, fold_v, None)
    queries_raw = qk[:, :q_cols]
    unrotated_keys = qk[:, q_cols:]
    own_places = lax.dynamic_slice_in_dim(positions, seq_at * tok_rows, tok_rows, 0)
    reach = (LOOKBACK_SPAN - 2) // tok_rows + 1

    def attend(query_matrix, stacked, key_places, valid):
        key_matrix = stacked[0].reshape(-1, local_kv, head_dim)
        value_matrix = stacked[1].reshape(-1, local_kv, head_dim)
        scores = (
            jnp.einsum(
                "qkgd,skd->kgqs", query_matrix, key_matrix, preferred_element_type=jnp.float32
            )
            * score_scale
        )
        distance = own_places[:, None] - key_places[None, :]
        allowed = valid[None, :] & (distance >= 0) & (distance < LOOKBACK_SPAN)
        weights = jnp.where(allowed[None, None], jnp.exp(scores), jnp.zeros_like(scores))
        total = jnp.sum(weights, axis=-1)
        summed = jnp.einsum(
            "kgqs,skd->qkgd",
            weights.astype(jnp.bfloat16),
            value_matrix,
            preferred_element_type=jnp.float32,
        )
        return (total, summed)

    key_matrix = rotary(
        norm_scale(unrotated_keys.reshape(tok_rows, local_kv, head_dim), key_gain), own_places
    )
    stacked = jnp.stack(
        [key_matrix.reshape(tok_rows, local_kv * head_dim), projected_values]
    ).astype(jnp.bfloat16)
    pieces = []
    for distance in range(reach, 0, -1):
        pieces.append(from_behind(stacked, SEQ, n_seq, distance))
    halo = jnp.concatenate(pieces, axis=1)
    query_matrix = rotary(
        norm_scale(queries_raw.reshape(tok_rows, local_kv * query_group, head_dim), query_gain),
        own_places,
    )
    query_matrix = query_matrix.astype(jnp.bfloat16).reshape(
        tok_rows, local_kv, query_group, head_dim
    )
    inner_total, inner_sum = attend(
        query_matrix, stacked, own_places, jnp.ones((tok_rows,), jnp.bool_)
    )
    span = halo.shape[1]
    padded_places = jnp.concatenate([jnp.zeros((span,), jnp.int32), positions])
    halo_places = lax.dynamic_slice_in_dim(padded_places, seq_at * tok_rows, span, 0)
    halo_valid = seq_at * tok_rows - span + jnp.arange(span, dtype=jnp.int32) >= 0
    outer_total, outer_sum = attend(query_matrix, halo, halo_places, halo_valid)
    total = jnp.transpose(inner_total + outer_total, (2, 0, 1))
    merged = (inner_sum + outer_sum) / total[..., None]
    attended = merged.astype(jnp.bfloat16).reshape(tok_rows, local_kv * query_group * head_dim)
    out_rel = jnp.zeros((tok_rows, ny, nx, nz, shard_rows), jnp.bfloat16)
    for dx, lo, hi, piece in b_pieces:
        cols = lax.dot_general(
            attended,
            piece[..., v_cols:],
            (((1,), (3,)), ((), ())),
            preferred_element_type=jnp.float32,
        )
        out_rel = out_rel.at[:, lo:hi, dx].set(cols.astype(jnp.bfloat16))
    out_abs = jnp.roll(out_rel, at_y, axis=1)
    out_abs = jnp.roll(out_abs, at_x, axis=2)
    out_abs = jnp.roll(out_abs, at_zh, axis=3)
    partial_out = out_abs.transpose(0, 3, 1, 2, 4).reshape(tok_rows, n_seq * shard_rows)
    summed_cols = reduce_scatter_tp(partial_out, dict(TP_PARTS)["zl"])
    full_width = post_gain.shape[0]
    own_squares = jnp.sum(summed_cols * summed_cols, axis=1)
    pair_squares = own_squares + lax.ppermute(own_squares, "c", [(0, 1), (1, 0)])
    squares = pair_squares
    n_zl = dict(TP_PARTS)["zl"]
    step = 1
    while step < n_zl:
        squares = squares + lax.ppermute(squares, "zl", [(i, i ^ step) for i in range(n_zl)])
        step *= 2
    inverse_rms = lax.rsqrt(squares / full_width + epsilon)
    gain_part = lax.dynamic_slice_in_dim(
        post_gain, tp_at * summed_cols.shape[1], summed_cols.shape[1], 0
    )
    return (residual.astype(jnp.float32) + summed_cols * inverse_rms[:, None] * gain_part).astype(
        jnp.bfloat16
    )


def solution(mesh):
    seq_n, tp_n = mesh.devices.shape
    shape = tuple(n for _, n in SEQ_PARTS) + tuple(n for _, n in TP_PARTS)
    assert int(np.prod(shape[:3])) == seq_n and int(np.prod(shape[3:])) == tp_n
    fine = Mesh(mesh.devices.reshape(shape), SEQ + TP)
    blocked = P(SEQ, TP)
    in_specs = (
        blocked,
        P(),
        blocked,
        blocked,
        blocked,
        P(),
        P(),
        P(TP, SEQ),
        P(),
        P(),
    )
    return jax.shard_map(local, mesh=fine, in_specs=in_specs, out_specs=blocked, check_vma=False)
```

```python
import jax
import jax.numpy as jnp
import numpy as np
from jax import lax
from jax.sharding import Mesh
from jax.sharding import PartitionSpec as P

LOOKBACK_SPAN = 1024

SEQ_PARTS = (("zh", 2), ("y", 8), ("x", 4))
TP_PARTS = (("zl", 4), ("c", 2))
SEQ = tuple(name for name, _ in SEQ_PARTS)
TP = tuple(name for name, _ in TP_PARTS)

epsilon = 1e-06
score_scale = 168.0 ** (-0.5)
rotary_base = 10000.0


def from_behind(block, axis, n, distance):
    route = [(i - distance, i) for i in range(n) if i - distance >= 0]
    return lax.ppermute(block, axis, route)


def ring(block, axis, n, split_axis):
    if n == 1:
        return [block]
    fwd = [(i, (i + 1) % n) for i in range(n)]
    bwd = [(i, (i - 1) % n) for i in range(n)]
    if n == 2:
        return [block, lax.ppermute(block, axis, fwd)]
    out = [None] * n
    out[0] = block
    left, right = block, block
    for d in range(1, (n + 1) // 2):
        left = lax.ppermute(left, axis, fwd)
        right = lax.ppermute(right, axis, bwd)
        out[n - d] = left
        out[d] = right
    if n % 2 == 0:
        k = block.shape[split_axis] // 2
        top = lax.ppermute(lax.slice_in_dim(left, 0, k, axis=split_axis), axis, fwd)
        bottom = lax.ppermute(lax.slice_in_dim(right, k, None, axis=split_axis), axis, bwd)
        out[n // 2] = (top, bottom)
    return out


def stacked_ring(block, axis, n, split_axis):
    parts = ring(block, axis, n, split_axis)
    whole = [jnp.concatenate(p, axis=split_axis) if isinstance(p, tuple) else p for p in parts]
    return jnp.stack(whole, axis=0)


def stacked_direct(block, axis, n):
    parts = [block] + [
        lax.ppermute(block, axis, [(j, (j - d) % n) for j in range(n)]) for d in range(1, n)
    ]
    return jnp.stack(parts, axis=0)


def ring_pieces(block, axis, n, split_axis, fold=None, acc=None):
    fwd = [(i, (i + 1) % n) for i in range(n)]
    bwd = [(i, (i - 1) % n) for i in range(n)]
    full = block.shape[split_axis]
    pieces = []

    def take(new):
        nonlocal acc
        pieces.extend(new)
        if fold is not None:
            acc = fold(acc, new)

    take([(0, 0, full, block)])
    left, right = block, block
    for d in range(1, (n + 1) // 2):
        if d > 1 and fold is not None:
            left, right, acc = lax.optimization_barrier((left, right, acc))
        left = lax.ppermute(left, axis, fwd)
        right = lax.ppermute(right, axis, bwd)
        take([(n - d, 0, full, left), (d, 0, full, right)])
    if n % 2 == 0:
        if fold is not None:
            left, right, acc = lax.optimization_barrier((left, right, acc))
        k = full // 2
        top = lax.ppermute(lax.slice_in_dim(left, 0, k, axis=split_axis), axis, fwd)
        bottom = lax.ppermute(lax.slice_in_dim(right, k, None, axis=split_axis), axis, bwd)
        take([(n // 2, 0, k, top), (n // 2, k, full, bottom)])
    return pieces, acc


def reduce_scatter_tp(partial, n_chip):
    rows = partial.shape[0]
    block_cols = partial.shape[1] // (2 * n_chip)
    at_c = lax.axis_index("c")
    at_z = lax.axis_index("zl")
    blocks = partial.reshape(rows, n_chip, 2, block_cols)
    keep = lax.dynamic_index_in_dim(blocks, at_c, axis=2, keepdims=False)
    give = lax.dynamic_index_in_dim(blocks, 1 - at_c, axis=2, keepdims=False)
    got = lax.ppermute(give, "c", [(0, 1), (1, 0)])
    chip_sum = keep.astype(jnp.float32) + got.astype(jnp.float32)
    total = lax.dynamic_index_in_dim(chip_sum, at_z, axis=1, keepdims=False)
    for d in range(1, n_chip):
        for sign in (1, -1):
            route = [(i, i + sign * d) for i in range(n_chip) if 0 <= i + sign * d < n_chip]
            target = jnp.clip(at_z + sign * d, 0, n_chip - 1)
            block = lax.dynamic_index_in_dim(chip_sum, target, axis=1, keepdims=False)
            total = total + lax.ppermute(block.astype(jnp.bfloat16), "zl", route).astype(jnp.float32)
    return total


def norm_scale(value_matrix, gain):
    mean_square = jnp.mean(value_matrix * value_matrix, axis=-1, keepdims=True)
    return value_matrix * lax.rsqrt(mean_square + epsilon) * gain


def rotary(value_matrix, places):
    half_dim = value_matrix.shape[-1] // 2
    inverse = rotary_base ** (-jnp.arange(half_dim, dtype=jnp.float32) / half_dim)
    angles = places.astype(jnp.float32)[:, None] * inverse[None, :]
    cosine = jnp.cos(angles)[:, None, :]
    sine = jnp.sin(angles)[:, None, :]
    first = value_matrix[..., :half_dim]
    second = value_matrix[..., half_dim:]
    return jnp.concatenate(
        [first * cosine - second * sine, second * cosine + first * sine], axis=-1
    )


def local(
    residual,
    input_gain,
    w_query,
    key_weight,
    value_weight,
    query_gain,
    key_gain,
    w_out,
    post_gain,
    positions,
):
    sizes = dict(SEQ_PARTS)
    n_seq = int(np.prod([n for _, n in SEQ_PARTS]))
    tok_rows = residual.shape[0]
    seq_at = lax.axis_index(SEQ)
    tp_at = lax.axis_index(TP)
    head_dim = query_gain.shape[0]
    local_kv = key_weight.shape[1] // head_dim
    query_group = w_query.shape[1] // key_weight.shape[1]
    q_cols = w_query.shape[1]
    k_cols = key_weight.shape[1]
    v_cols = value_weight.shape[1]
    shard_rows = w_query.shape[0]

    nz, ny, nx = sizes["zh"], sizes["y"], sizes["x"]
    gathered = lax.all_gather(residual, TP, axis=1, tiled=True)
    normalized_input = norm_scale(gathered.astype(jnp.float32), input_gain).astype(jnp.bfloat16)
    at_zh, at_y, at_x = (lax.axis_index(name) for name in SEQ)
    normed_rel = normalized_input.reshape(tok_rows, nz, ny, nx, shard_rows).transpose(0, 2, 3, 1, 4)
    normed_rel = jnp.roll(normed_rel, -at_y, axis=1)
    normed_rel = jnp.roll(normed_rel, -at_x, axis=2)
    normed_rel = jnp.roll(normed_rel, -at_zh, axis=3)

    def contract(lhs, piece):
        return lax.dot_general(
            lhs, piece, (((1, 2, 3), (0, 1, 2)), ((), ())), preferred_element_type=jnp.float32
        )

    def fold_qk(acc, new):
        for dy, lo, hi, piece in new:
            term = contract(normed_rel[:, dy, :, lo:hi], piece)
            acc = term if acc is None else acc + term
        return acc

    def fold_v(acc, new):
        for dx, lo, hi, piece in new:
            term = contract(normed_rel[:, :, dx, lo:hi], piece)
            acc = term if acc is None else acc + term
        return acc

    packed = jnp.concatenate([w_query, key_weight, value_weight, w_out.T], axis=1)
    by_zh = stacked_ring(packed, "zh", nz, 0)
    split = q_cols + k_cols
    half_a = by_zh[:, :, :split]
    half_b = by_zh[:, :, split:]
    a_x = stacked_direct(half_a, "x", nx)
    b_y = stacked_ring(half_b, "y", ny, 0)
    _, qk = ring_pieces(a_x, "y", ny, 1, fold_qk, None)
    b_pieces, b_sum = ring_pieces(b_y, "x", nx, 1, fold_v, None)
    projected_values = b_sum[:, :v_cols]
    queries_raw = qk[:, :q_cols]
    unrotated_keys = qk[:, q_cols:]
    own_places = lax.dynamic_slice_in_dim(positions, seq_at * tok_rows, tok_rows, 0)
    reach = (LOOKBACK_SPAN - 2) // tok_rows + 1

    def attend(query_matrix, stacked, key_places, valid):
        key_matrix = stacked[0].reshape(-1, local_kv, head_dim)
        value_matrix = stacked[1].reshape(-1, local_kv, head_dim)
        scores = (
            jnp.einsum(
                "qkgd,skd->kgqs", query_matrix, key_matrix, preferred_element_type=jnp.float32
            )
            * score_scale
        )
        distance = own_places[:, None] - key_places[None, :]
        allowed = valid[None, :] & (distance >= 0) & (distance < LOOKBACK_SPAN)
        weights = jnp.where(allowed[None, None], jnp.exp(scores), jnp.zeros_like(scores))
        total = jnp.sum(weights, axis=-1)
        summed = jnp.einsum(
            "kgqs,skd->qkgd",
            weights.astype(jnp.bfloat16),
            value_matrix,
            preferred_element_type=jnp.float32,
        )
        return (total, summed)

    key_matrix = rotary(
        norm_scale(unrotated_keys.reshape(tok_rows, local_kv, head_dim), key_gain), own_places
    )
    stacked = jnp.stack(
        [key_matrix.reshape(tok_rows, local_kv * head_dim), projected_values]
    ).astype(jnp.bfloat16)
    pieces = []
    for distance in range(reach, 0, -1):
        pieces.append(from_behind(stacked, SEQ, n_seq, distance))
    halo = jnp.concatenate(pieces, axis=1)
    query_matrix = rotary(
        norm_scale(queries_raw.reshape(tok_rows, local_kv * query_group, head_dim), query_gain),
        own_places,
    )
    query_matrix = query_matrix.astype(jnp.bfloat16).reshape(
        tok_rows, local_kv, query_group, head_dim
    )
    inner_total, inner_sum = attend(
        query_matrix, stacked, own_places, jnp.ones((tok_rows,), jnp.bool_)
    )
    span = halo.shape[1]
    padded_places = jnp.concatenate([jnp.zeros((span,), jnp.int32), positions])
    halo_places = lax.dynamic_slice_in_dim(padded_places, seq_at * tok_rows, span, 0)
    halo_valid = seq_at * tok_rows - span + jnp.arange(span, dtype=jnp.int32) >= 0
    outer_total, outer_sum = attend(query_matrix, halo, halo_places, halo_valid)
    total = jnp.transpose(inner_total + outer_total, (2, 0, 1))
    merged = (inner_sum + outer_sum) / total[..., None]
    attended = merged.astype(jnp.bfloat16).reshape(tok_rows, local_kv * query_group * head_dim)
    out_rel = jnp.zeros((tok_rows, ny, nx, nz, shard_rows), jnp.bfloat16)
    attended_wide = jnp.concatenate(
        [jnp.zeros((tok_rows, v_cols), attended.dtype), attended], axis=1
    )
    for dx, lo, hi, piece in b_pieces:
        cols = lax.dot_general(
            attended_wide,
            piece,
            (((1,), (3,)), ((), ())),
            preferred_element_type=jnp.float32,
        )
        out_rel = out_rel.at[:, :, dx, lo:hi].set(cols.astype(jnp.bfloat16))
    out_abs = jnp.roll(out_rel, at_y, axis=1)
    out_abs = jnp.roll(out_abs, at_x, axis=2)
    out_abs = jnp.roll(out_abs, at_zh, axis=3)
    partial_out = out_abs.transpose(0, 3, 1, 2, 4).reshape(tok_rows, n_seq * shard_rows)
    summed_cols = reduce_scatter_tp(partial_out, dict(TP_PARTS)["zl"])
    full_width = post_gain.shape[0]
    own_squares = jnp.sum(summed_cols * summed_cols, axis=1)
    pair_squares = own_squares + lax.ppermute(own_squares, "c", [(0, 1), (1, 0)])
    squares = lax.psum(pair_squares, "zl")
    inverse_rms = lax.rsqrt(squares / full_width + epsilon)
    gain_part = lax.dynamic_slice_in_dim(
        post_gain, tp_at * summed_cols.shape[1], summed_cols.shape[1], 0
    )
    return (residual.astype(jnp.float32) + summed_cols * inverse_rms[:, None] * gain_part).astype(
        jnp.bfloat16
    )


def solution(mesh):
    seq_n, tp_n = mesh.devices.shape
    shape = tuple(n for _, n in SEQ_PARTS) + tuple(n for _, n in TP_PARTS)
    assert int(np.prod(shape[:3])) == seq_n and int(np.prod(shape[3:])) == tp_n
    fine = Mesh(mesh.devices.reshape(shape), SEQ + TP)
    blocked = P(SEQ, TP)
    in_specs = (
        blocked,
        P(),
        blocked,
        blocked,
        blocked,
        P(),
        P(),
        P(TP, SEQ),
        P(),
        P(),
    )
    return jax.shard_map(local, mesh=fine, in_specs=in_specs, out_specs=blocked, check_vma=False)
```
